256 devices in a mesh: ctx: 8 (over z), head: 16 (over y, x), req: 2 (over core).
Axes of the slice: x: 4, y: 4, z: 8, core: 2. Of those that a mesh axis runs over, the one named last changes fastest.
Arguments:
- x_in: bfloat16 [2, 8192, 16384], P('req', 'ctx', 'head'), may hold values from -6 to 6
- bc_in: bfloat16 [2, 8192, 4096], P('req', 'ctx'), may hold values from -0.625 to 0.625
- z_in: bfloat16 [2, 8192, 16384], P('req', 'ctx', 'head'), may hold values from -6 to 6
- dt_raw: float32 [2, 256, 8192], P('req', 'head', 'ctx'), may hold values from -6 to 6
- dt_bias: float32 [256], P('head'), may hold values from -3 to 1
- decay_rate: float32 [256], P('head'), may hold values from 1e-06 to 0.05
- skip_gain: float32 [256], P('head'), may hold values from 0.5 to 1.5
- conv_x: float32 [4, 16384], P(None, 'head'), may hold values from -3 to 3
- conv_bc: float32 [4, 4096], replicated, may hold values from -3 to 3
- ssm_pool: float32 [16, 256, 64, 256], P(('ctx', 'req'), 'head'), may hold values from -6 to 6
- conv_pool: float32 [16, 3, 16384], P(('ctx', 'req'), None, 'head'), may hold values from -6 to 6
- bc_cache: float32 [2, 3, 4096], P('req'), may hold values from -0.625 to 0.625
- owner: int32 [2, 16], P(None, 'head'), may hold values from 0 to 15, as said below
- lengths: int32 [2], replicated, may hold values from 2048 to 8192, as said below
Outputs:
- y_out: bfloat16 [2, 8192, 16384], P('req', 'ctx', 'head')
- block_states: float32 [2, 8, 256, 64, 256], P('req', 'ctx', 'head')
The draws below stay inside these ranges and needn't reach their ends.
Inputs may be any that keep to these rules, and one draw needn't show every extreme that they name: `owner`: for every head block the requests' cached states lie in different slots. `lengths`: one request has all 8192 new tokens.
All inputs are finite; a program needn't handle non-finite values.
Results may differ from the reference program's by a relative error of at most 0.0053.
Values may be sent and summed in bfloat16 or wider, within the bound.
No kernel may reach another device: no remote copies, remote signals or barrier semaphores. Data moves between devices by JAX's collectives and lax.ppermute only.
A program may use at most 128 MiB of HBM per device.

```python
import math
from functools import partial
import jax
import jax.numpy as jnp
from jax import lax

H = 256
P_SIZE = 64
N = 256
G = 8
K = 4
STRETCH = 256
L_DEV = 1024
TOK = 8192
REQS = 2
SLOTS = 16
CTX_BLOCKS = 8
HEAD_BLOCKS = 16


def draw_owner(key, part):
    first_key, stride_key = jax.random.split(key)
    base_slot = jax.random.randint(first_key, (HEAD_BLOCKS,), 0, SLOTS)
    stride = jax.random.randint(stride_key, (HEAD_BLOCKS,), 1, SLOTS // REQS + 1)
    offsets = jnp.arange(REQS, dtype=jnp.int32)[:, None] * stride[None, :]
    return ((base_slot[None, :] + offsets) % SLOTS).astype(jnp.int32)


def draw_lengths(key, part):
    pick_key, length_key = jax.random.split(key)
    full_one = jax.random.randint(pick_key, (), 0, REQS)
    others = jax.random.randint(length_key, (REQS,), TOK // 4, TOK + 1)
    return jnp.where(jnp.arange(REQS) == full_one, TOK, others).astype(jnp.int32)


def level_of(key, dims, shards, low, largest):
    def one(position, blocks):
        draws = jax.random.uniform(jax.random.fold_in(jax.random.fold_in(key, 6), position), (blocks,), jnp.float32, low / len(shards), largest / len(shards))
        return jnp.repeat(jnp.exp(draws), dims[position] // blocks).reshape((-1,) + (1,) * (len(dims) - position - 1))

    level = one(*shards[0])
    for cut in shards[1:]:
        level = level * one(*cut)
    return level


def gaussian(own_key, dims, scale, limit, shards=(), held_as=jnp.bfloat16):
    drawn = scale * jax.random.normal(own_key, dims, jnp.float32)
    if shards:
        drawn = drawn * level_of(own_key, dims, shards, -0.22, 0.18)
    return jnp.clip(drawn, -limit, limit).astype(held_as)


def setup_inputs(seed: int = 0) -> dict:
    keys = jax.random.split(jax.random.key(seed), 15)
    x_in = gaussian(keys[0], (REQS, TOK, H * P_SIZE), 1.0, 6.0, ((0, 2), (1, 8), (2, 16)))
    bc_in = gaussian(keys[1], (REQS, TOK, 2 * G * N), 0.1, 0.625, ((0, 2), (1, 8)))
    z_in = gaussian(keys[2], (REQS, TOK, H * P_SIZE), 1.0, 6.0, ((0, 2), (1, 8), (2, 16)))
    dt_raw = gaussian(keys[3], (REQS, H, TOK), 1.0, 6.0, ((0, 2), (1, 16), (2, 8)), jnp.float32)
    dt_bias = jnp.clip(-3.0 + 4.0 * jax.random.uniform(keys[4], (H,), jnp.float32) ** level_of(keys[4], (H,), ((0, 16),), -0.2, 0.2), -3.0, 1.0)
    decay_rate = jnp.clip(jnp.exp(math.log(0.05) - 10.819778 * jax.random.uniform(keys[5], (H,), jnp.float32) ** level_of(keys[5], (H,), ((0, 16),), -0.2, 0.2)), 9.999999974752427e-07, 0.05)
    skip_gain = jnp.clip(0.5 + 1.0 * jax.random.uniform(keys[6], (H,), jnp.float32) ** level_of(keys[6], (H,), ((0, 16),), -0.2, 0.2), 0.5, 1.5)
    conv_x = gaussian(keys[7], (K, H * P_SIZE), K ** -0.5, 3.0, ((1, 16),), jnp.float32)
    conv_bc = gaussian(keys[8], (K, 2 * G * N), K ** -0.5, 3.0, (), jnp.float32)
    ssm_pool = gaussian(keys[9], (SLOTS, H, P_SIZE, N), 1.0, 6.0, ((0, 16), (1, 16)), jnp.float32)
    conv_pool = gaussian(keys[10], (SLOTS, K - 1, H * P_SIZE), 1.0, 6.0, ((0, 16), (2, 16)), jnp.float32)
    bc_cache = gaussian(keys[11], (REQS, K - 1, 2 * G * N), 0.1, 0.625, ((0, 2),), jnp.float32)
    owner = draw_owner(jax.random.fold_in(keys[14], 71), 0)
    lengths = draw_lengths(jax.random.fold_in(keys[14], 71), 0)
    return {"x_in": x_in, "bc_in": bc_in, "z_in": z_in, "dt_raw": dt_raw, "dt_bias": dt_bias, "decay_rate": decay_rate, "skip_gain": skip_gain, "conv_x": conv_x, "conv_bc": conv_bc, "ssm_pool": ssm_pool, "conv_pool": conv_pool, "bc_cache": bc_cache, "owner": owner, "lengths": lengths}


HIGHEST = lax.Precision.HIGHEST


def causal_conv(prev_rows, rows, taps):
    padded = jnp.concatenate([prev_rows, rows.astype(jnp.float32)], axis=0)
    count = rows.shape[0]
    total = taps[0] * padded[0:count]
    for offset in range(1, taps.shape[0]):
        total = total + taps[offset] * padded[offset:offset + count]
    return jax.nn.silu(total).astype(jnp.bfloat16)


def block_step(running, pieces, skip_gain):
    x_blk, b_blk, c_blk, step_blk, log_blk = pieces
    cum = jnp.cumsum(log_blk, axis=1)
    block_len = x_blk.shape[0]
    head_count = x_blk.shape[1]
    scores = jnp.einsum("qgn,sgn->gqs", c_blk.astype(jnp.float32), b_blk.astype(jnp.float32))
    group_count = scores.shape[0]
    per_group = head_count // group_count
    scores_h = jnp.broadcast_to(scores[:, None], (group_count, per_group, block_len, block_len)).reshape(head_count, block_len, block_len)
    row_ids = lax.broadcasted_iota(jnp.int32, (block_len, block_len), 0)
    col_ids = lax.broadcasted_iota(jnp.int32, (block_len, block_len), 1)
    causal = (row_ids >= col_ids)[None]
    decay_gap = jnp.where(causal, cum[:, :, None] - cum[:, None, :], 0.0)
    decay_mask = jnp.where(causal, jnp.exp(-decay_gap), 0.0)
    weights = (scores_h * decay_mask * step_blk[:, None, :]).astype(jnp.bfloat16)
    y_intra = jnp.einsum("hqs,shp->qhp", weights.astype(jnp.float32), x_blk.astype(jnp.float32))
    state_view = running.reshape(group_count, per_group, running.shape[1], running.shape[2])
    y_state = jnp.einsum("qgn,gjpn->qgjp", c_blk.astype(jnp.float32), state_view, precision=HIGHEST)
    y_state = y_state.reshape(block_len, head_count, running.shape[1]) * jnp.exp(-cum).T[:, :, None]
    block_out = y_intra + y_state + skip_gain[None, :, None] * x_blk.astype(jnp.float32)
    block_end = cum[:, -1:]
    factor = step_blk * jnp.exp(-(block_end - cum))
    weighted = (x_blk.astype(jnp.float32) * factor.T[:, :, None]).astype(jnp.bfloat16)
    weighted_view = weighted.reshape(block_len, group_count, per_group, running.shape[1])
    contrib = jnp.einsum("qgjp,qgn->gjpn", weighted_view.astype(jnp.float32), b_blk.astype(jnp.float32)).reshape(running.shape)
    running = jnp.exp(-cum[:, -1])[:, None, None] * running + contrib
    return running, block_out


def reference(x_in, bc_in, z_in, dt_raw, dt_bias, decay_rate, skip_gain, conv_x, conv_bc, ssm_pool, conv_pool, bc_cache, owner, lengths):
    per_block = H // HEAD_BLOCKS
    per_dev = L_DEV // STRETCH
    block_ids = jnp.arange(HEAD_BLOCKS, dtype=jnp.int32)
    results = []
    saved = []
    for request in range(REQS):
        owners = owner[request]
        pool_view = ssm_pool.reshape(SLOTS, HEAD_BLOCKS, per_block, P_SIZE, N)
        init_state = pool_view[owners, block_ids].reshape(H, P_SIZE, N)
        conv_view = conv_pool.reshape(SLOTS, K - 1, HEAD_BLOCKS, per_block * P_SIZE)
        conv_prefix = jnp.transpose(conv_view[owners, :, block_ids], (1, 0, 2)).reshape(K - 1, H * P_SIZE)
        x_conv = causal_conv(conv_prefix, x_in[request], conv_x)
        bc_conv = causal_conv(bc_cache[request], bc_in[request], conv_bc)
        b_all = bc_conv[:, :G * N].reshape(CTX_BLOCKS, per_dev, STRETCH, G, N)
        c_all = bc_conv[:, G * N:].reshape(CTX_BLOCKS, per_dev, STRETCH, G, N)
        positions = jnp.arange(TOK, dtype=jnp.int32)
        live_mask = (positions < lengths[request]).astype(jnp.float32)
        step_size = jax.nn.softplus(dt_raw[request] + dt_bias[:, None]) * live_mask[None, :]
        log_decay = step_size * decay_rate[:, None]
        step_view = step_size.reshape(H, CTX_BLOCKS, per_dev, STRETCH).transpose(1, 2, 0, 3)
        log_view = log_decay.reshape(H, CTX_BLOCKS, per_dev, STRETCH).transpose(1, 2, 0, 3)
        x_view = x_conv.reshape(CTX_BLOCKS, per_dev, STRETCH, H, P_SIZE)
        inner = partial(block_step, skip_gain=skip_gain)

        def token_block(running, pieces):
            running, outputs = lax.scan(inner, running, pieces)
            return running, (outputs, running)

        _, (mixed, block_end_states) = lax.scan(token_block, init_state, (x_view, b_all, c_all, step_view, log_view))
        mixed = mixed.reshape(TOK, H, P_SIZE)
        gate_act = jax.nn.silu(z_in[request].astype(jnp.float32)).reshape(TOK, H, P_SIZE)
        gated = (mixed * gate_act * live_mask[:, None, None]).reshape(TOK, H * P_SIZE).astype(jnp.bfloat16)
        results.append(gated)
        saved.append(block_end_states)
    return jnp.stack(results), jnp.stack(saved)
```

```python
from functools import partial

import jax
import jax.numpy as jnp
from jax import lax
from jax.sharding import PartitionSpec as P

H = 256
P_SIZE = 64
N = 256
G = 8
K = 4
STRETCH = 256
CHUNKS = 4


HIGHEST = lax.Precision.HIGHEST


def passed_along(value, axis, steps):
    count = lax.axis_size(axis)
    initial, last = (max(0, -steps), min(count, count - steps))
    return lax.ppermute(value, axis, [(source, source + steps) for source in range(initial, last)])


def causal_conv(prev_rows, rows, taps):
    padded = jnp.concatenate([prev_rows, rows.astype(jnp.float32)], axis=0)
    count = rows.shape[0]
    total = taps[0] * padded[0:count]
    for offset in range(1, taps.shape[0]):
        total = total + taps[offset] * padded[offset : offset + count]
    return jax.nn.silu(total).astype(jnp.bfloat16)


def block_state(running, x_blk, b_blk, step_blk, cum):
    block_len, head_count = x_blk.shape[0], x_blk.shape[1]
    group_count = b_blk.shape[1]
    per_group = head_count // group_count
    block_end = cum[:, -1:]
    factor = step_blk * jnp.exp(-(block_end - cum))
    weighted = (x_blk.astype(jnp.float32) * factor.T[:, :, None]).astype(jnp.bfloat16)
    weighted_view = weighted.reshape(block_len, group_count, per_group, running.shape[1])
    contrib = jnp.einsum(
        "qgjp,qgn->gjpn", weighted_view, b_blk, preferred_element_type=jnp.float32
    ).reshape(running.shape)
    return jnp.exp(-cum[:, -1])[:, None, None] * running + contrib


def block_output(running, x_blk, b_blk, c_blk, step_blk, cum, skip_gain):
    block_len = x_blk.shape[0]
    head_count = x_blk.shape[1]
    scores = jnp.einsum("qgn,sgn->gqs", c_blk, b_blk, preferred_element_type=jnp.float32)
    group_count = scores.shape[0]
    per_group = head_count // group_count
    scores_h = jnp.broadcast_to(
        scores[:, None], (group_count, per_group, block_len, block_len)
    ).reshape(head_count, block_len, block_len)
    row_ids = lax.broadcasted_iota(jnp.int32, (block_len, block_len), 0)
    col_ids = lax.broadcasted_iota(jnp.int32, (block_len, block_len), 1)
    causal = (row_ids >= col_ids)[None]
    decay_gap = jnp.where(causal, cum[:, :, None] - cum[:, None, :], 0.0)
    decay_mask = jnp.where(causal, jnp.exp(-decay_gap), 0.0)
    weights = (scores_h * decay_mask * step_blk[:, None, :]).astype(jnp.bfloat16)
    y_intra = jnp.einsum("hqs,shp->qhp", weights, x_blk, preferred_element_type=jnp.float32)
    state_view = running.reshape(group_count, per_group, running.shape[1], running.shape[2])
    y_state = jnp.einsum("qgn,gjpn->qgjp", c_blk.astype(jnp.float32), state_view, precision=HIGHEST)
    y_state = y_state.reshape(block_len, head_count, running.shape[1]) * jnp.exp(-cum).T[:, :, None]
    return y_intra + y_state + skip_gain[None, :, None] * x_blk.astype(jnp.float32)


def on_device(
    x_in,
    bc_in,
    z_in,
    dt_raw,
    dt_bias,
    decay_rate,
    skip_gain,
    conv_x,
    conv_bc,
    ssm_pool,
    conv_pool,
    bc_cache,
    owner,
    lengths,
):
    n_ctx = lax.axis_size("ctx")
    n_req = lax.axis_size("req")
    ctx_pos = lax.axis_index("ctx")
    head_pos = lax.axis_index("head")
    req_pos = lax.axis_index("req")
    local_heads = dt_raw.shape[1]
    tokens = x_in.shape[1]
    at_start = ctx_pos == 0

    want = owner[req_pos, 0]
    on_chip = (want // n_req) == ctx_pos
    pick = want % n_req
    swap = [(src, n_req - 1 - src) for src in range(n_req)]
    other_pool, other_conv = lax.ppermute((ssm_pool[0], conv_pool[0]), "req", swap)
    mine = pick == req_pos
    first_conv = lax.psum(
        jnp.where(on_chip, jnp.where(mine, conv_pool[0], other_conv), 0.0), "ctx"
    )
    first_state = lax.psum(
        jnp.where(on_chip, jnp.where(mine, ssm_pool[0], other_pool), 0.0), "ctx"
    )

    tail_x = x_in[0, tokens - (K - 1) :, :]
    tail_bc = bc_in[0, tokens - (K - 1) :, :]
    prev_x, prev_bc = passed_along((tail_x, tail_bc), "ctx", 1)
    prev_x = jnp.where(at_start, first_conv, prev_x.astype(jnp.float32))
    prev_bc = jnp.where(at_start, bc_cache[0], prev_bc.astype(jnp.float32))
    per_group = H // G
    local_groups = max(1, local_heads // per_group)
    group_start = head_pos * local_heads // per_group
    span = local_groups * N

    def pick_groups(values):
        input_cols = lax.dynamic_slice_in_dim(values, group_start * N, span, 1)
        output_cols = lax.dynamic_slice_in_dim(values, G * N + group_start * N, span, 1)
        return jnp.concatenate([input_cols, output_cols], axis=1)

    x_conv = causal_conv(prev_x, x_in[0], conv_x)
    bc_conv = causal_conv(pick_groups(prev_bc), pick_groups(bc_in[0]), pick_groups(conv_bc))
    positions = ctx_pos * tokens + lax.iota(jnp.int32, tokens)
    live_mask = (positions < lengths[req_pos]).astype(jnp.float32)
    step_size = jax.nn.softplus(dt_raw[0] + dt_bias[:, None]) * live_mask[None, :]
    log_decay = step_size * decay_rate[:, None]
    blocks = tokens // STRETCH
    x_view = x_conv.reshape(blocks, STRETCH, local_heads, P_SIZE)
    b_view = bc_conv[:, :span].reshape(blocks, STRETCH, local_groups, N)
    c_view = bc_conv[:, span:].reshape(blocks, STRETCH, local_groups, N)
    step_view = step_size.reshape(local_heads, blocks, STRETCH).transpose(1, 0, 2)
    log_view = log_decay.reshape(local_heads, blocks, STRETCH).transpose(1, 0, 2)
    cum_view = jnp.cumsum(log_view, axis=2)

    running = jnp.zeros((local_heads, P_SIZE, N), jnp.float32)
    starts = []
    for blk in range(blocks):
        starts.append(running)
        running = block_state(running, x_view[blk], b_view[blk], step_view[blk], cum_view[blk])
    local_end = running
    own_decay = jnp.exp(-jnp.sum(log_decay, axis=1))

    chunk = local_heads // CHUNKS
    end_chunks = local_end.reshape(CHUNKS, chunk, P_SIZE, N)
    decay_chunks = own_decay.reshape(CHUNKS, chunk)
    got = jnp.zeros((chunk, P_SIZE, N), jnp.float32)
    received = []
    for step in range(n_ctx + CHUNKS - 2):
        index = jnp.clip(step - ctx_pos, 0, CHUNKS - 1)
        sent = (
            lax.dynamic_index_in_dim(decay_chunks, index, keepdims=False)[:, None, None] * got
            + lax.dynamic_index_in_dim(end_chunks, index, keepdims=False)
        )
        pairs = [
            (src, src + 1)
            for src in range(max(0, step - CHUNKS + 1), min(step, n_ctx - 2) + 1)
        ]
        got = lax.ppermute(sent, "ctx", pairs)
        received.append(got)
    received = jnp.stack(received)
    prefix = lax.dynamic_slice_in_dim(received, jnp.maximum(ctx_pos - 1, 0), CHUNKS, 0)
    prefix = jnp.where(at_start, 0.0, prefix.reshape(local_heads, P_SIZE, N))

    all_decay = lax.all_gather(own_decay, "ctx")
    earlier = (lax.iota(jnp.int32, n_ctx) < ctx_pos)[:, None]
    decay_before = jnp.prod(jnp.where(earlier, all_decay, 1.0), axis=0)
    start_state = prefix + decay_before[:, None, None] * first_state
    end_state = own_decay[:, None, None] * start_state + local_end

    outs = []
    for blk in range(blocks):
        outs.append(
            block_output(
                starts[blk], x_view[blk], b_view[blk], c_view[blk], step_view[blk],
                cum_view[blk], skip_gain,
            )
        )
    local_out = jnp.concatenate(outs, axis=0)

    cum_dev = jnp.cumsum(log_decay, axis=1)
    readout = bc_conv[:, span:].reshape(tokens, local_groups, N)
    start_view = start_state.reshape(local_groups, local_heads // local_groups, P_SIZE, N)
    carried = jnp.einsum(
        "tgn,gjpn->tgjp", readout.astype(jnp.float32), start_view, precision=HIGHEST
    )
    carried = carried.reshape(tokens, local_heads, P_SIZE) * jnp.exp(-cum_dev).T[:, :, None]
    mixed = local_out + carried
    gate_act = jax.nn.silu(z_in[0].astype(jnp.float32)).reshape(tokens, local_heads, P_SIZE)
    gated = (
        (mixed * gate_act * live_mask[:, None, None])
        .reshape(1, tokens, local_heads * P_SIZE)
        .astype(jnp.bfloat16)
    )
    return (gated, end_state[None, None])


def solution(mesh):
    return jax.shard_map(
        on_device,
        mesh=mesh,
        in_specs=(
            P("req", "ctx", "head"),
            P("req", "ctx", None),
            P("req", "ctx", "head"),
            P("req", "head", "ctx"),
            P("head"),
            P("head"),
            P("head"),
            P(None, "head"),
            P(),
            P(("ctx", "req"), "head", None, None),
            P(("ctx", "req"), None, "head"),
            P("req", None, None),
            P(None, "head"),
            P(),
        ),
        out_specs=(P("req", "ctx", "head"), P("req", "ctx", "head", None, None)),
        check_vma=False,
    )
```

```python
from functools import partial

import jax
import jax.numpy as jnp
from jax import lax
from jax.sharding import PartitionSpec as P

H = 256
P_SIZE = 64
N = 256
G = 8
K = 4
STRETCH = 256
CHUNKS = 4


HIGHEST = lax.Precision.HIGHEST


def passed_along(value, axis, steps):
    count = lax.axis_size(axis)
    initial, last = (max(0, -steps), min(count, count - steps))
    return lax.ppermute(value, axis, [(source, source + steps) for source in range(initial, last)])


def causal_conv(prev_rows, rows, taps):
    padded = jnp.concatenate([prev_rows, rows.astype(jnp.float32)], axis=0)
    count = rows.shape[0]
    total = taps[0] * padded[0:count]
    for offset in range(1, taps.shape[0]):
        total = total + taps[offset] * padded[offset : offset + count]
    return jax.nn.silu(total).astype(jnp.bfloat16)


def block_state(running, x_blk, b_blk, step_blk, cum):
    block_len, head_count = x_blk.shape[0], x_blk.shape[1]
    group_count = b_blk.shape[1]
    per_group = head_count // group_count
    block_end = cum[:, -1:]
    factor = step_blk * jnp.exp(-(block_end - cum))
    weighted = (x_blk.astype(jnp.float32) * factor.T[:, :, None]).astype(jnp.bfloat16)
    weighted_view = weighted.reshape(block_len, group_count, per_group, running.shape[1])
    contrib = jnp.einsum(
        "qgjp,qgn->gjpn", weighted_view, b_blk, preferred_element_type=jnp.float32
    ).reshape(running.shape)
    return jnp.exp(-cum[:, -1])[:, None, None] * running + contrib


def block_output(running, x_blk, b_blk, c_blk, step_blk, cum, skip_gain):
    block_len = x_blk.shape[0]
    head_count = x_blk.shape[1]
    scores = jnp.einsum("qgn,sgn->gqs", c_blk, b_blk, preferred_element_type=jnp.float32)
    group_count = scores.shape[0]
    per_group = head_count // group_count
    scores_h = jnp.broadcast_to(
        scores[:, None], (group_count, per_group, block_len, block_len)
    ).reshape(head_count, block_len, block_len)
    row_ids = lax.broadcasted_iota(jnp.int32, (block_len, block_len), 0)
    col_ids = lax.broadcasted_iota(jnp.int32, (block_len, block_len), 1)
    causal = (row_ids >= col_ids)[None]
    decay_gap = jnp.where(causal, cum[:, :, None] - cum[:, None, :], 0.0)
    decay_mask = jnp.where(causal, jnp.exp(-decay_gap), 0.0)
    weights = (scores_h * decay_mask * step_blk[:, None, :]).astype(jnp.bfloat16)
    y_intra = jnp.einsum("hqs,shp->qhp", weights, x_blk, preferred_element_type=jnp.float32)
    state_view = running.reshape(group_count, per_group, running.shape[1], running.shape[2])
    y_state = jnp.einsum("qgn,gjpn->qgjp", c_blk.astype(jnp.float32), state_view, precision=HIGHEST)
    y_state = y_state.reshape(block_len, head_count, running.shape[1]) * jnp.exp(-cum).T[:, :, None]
    return y_intra + y_state + skip_gain[None, :, None] * x_blk.astype(jnp.float32)


def on_device(
    x_in,
    bc_in,
    z_in,
    dt_raw,
    dt_bias,
    decay_rate,
    skip_gain,
    conv_x,
    conv_bc,
    ssm_pool,
    conv_pool,
    bc_cache,
    owner,
    lengths,
):
    n_ctx = lax.axis_size("ctx")
    n_req = lax.axis_size("req")
    ctx_pos = lax.axis_index("ctx")
    head_pos = lax.axis_index("head")
    req_pos = lax.axis_index("req")
    local_heads = dt_raw.shape[1]
    tokens = x_in.shape[1]
    at_start = ctx_pos == 0

    want = owner[req_pos, 0]
    on_chip = (want // n_req) == ctx_pos
    pick = want % n_req
    swap = [(src, n_req - 1 - src) for src in range(n_req)]
    other_pool = lax.ppermute(ssm_pool[0], "req", swap)
    state_pick = jnp.where(
        on_chip, jnp.where(pick == req_pos, ssm_pool[0], other_pool), 0.0
    )
    state_pick, x_in = lax.optimization_barrier((state_pick, x_in))
    first_state = lax.psum(state_pick, "ctx")
    slot_pos = ctx_pos * n_req + req_pos
    conv_picks = jnp.stack(
        [jnp.where(owner[r, 0] == slot_pos, conv_pool[0], 0.0) for r in range(n_req)]
    )
    first_conv = lax.psum(conv_picks, ("ctx", "req"))[req_pos]

    tail_x = x_in[0, tokens - (K - 1) :, :]
    tail_bc = bc_in[0, tokens - (K - 1) :, :]
    prev_x, prev_bc = passed_along((tail_x, tail_bc), "ctx", 1)
    prev_x = jnp.where(at_start, first_conv, prev_x.astype(jnp.float32))
    prev_bc = jnp.where(at_start, bc_cache[0], prev_bc.astype(jnp.float32))
    per_group = H // G
    local_groups = max(1, local_heads // per_group)
    group_start = head_pos * local_heads // per_group
    span = local_groups * N

    def pick_groups(values):
        input_cols = lax.dynamic_slice_in_dim(values, group_start * N, span, 1)
        output_cols = lax.dynamic_slice_in_dim(values, G * N + group_start * N, span, 1)
        return jnp.concatenate([input_cols, output_cols], axis=1)

    x_conv = causal_conv(prev_x, x_in[0], conv_x)
    bc_conv = causal_conv(pick_groups(prev_bc), pick_groups(bc_in[0]), pick_groups(conv_bc))
    positions = ctx_pos * tokens + lax.iota(jnp.int32, tokens)
    live_mask = (positions < lengths[req_pos]).astype(jnp.float32)
    step_size = jax.nn.softplus(dt_raw[0] + dt_bias[:, None]) * live_mask[None, :]
    log_decay = step_size * decay_rate[:, None]
    blocks = tokens // STRETCH
    x_view = x_conv.reshape(blocks, STRETCH, local_heads, P_SIZE)
    b_view = bc_conv[:, :span].reshape(blocks, STRETCH, local_groups, N)
    c_view = bc_conv[:, span:].reshape(blocks, STRETCH, local_groups, N)
    step_view = step_size.reshape(local_heads, blocks, STRETCH).transpose(1, 0, 2)
    log_view = log_decay.reshape(local_heads, blocks, STRETCH).transpose(1, 0, 2)
    cum_view = jnp.cumsum(log_view, axis=2)

    running = jnp.zeros((local_heads, P_SIZE, N), jnp.float32)
    starts = []
    for blk in range(blocks):
        starts.append(running)
        running = block_state(running, x_view[blk], b_view[blk], step_view[blk], cum_view[blk])
    local_end = running
    own_decay = jnp.exp(-jnp.sum(log_decay, axis=1))

    chunk = local_heads // CHUNKS
    end_chunks = local_end.reshape(CHUNKS, chunk, P_SIZE, N)
    decay_chunks = own_decay.reshape(CHUNKS, chunk)
    got = jnp.zeros((chunk, P_SIZE, N), jnp.float32)
    received = []
    for step in range(n_ctx + CHUNKS - 2):
        index = jnp.clip(step - ctx_pos, 0, CHUNKS - 1)
        sent = (
            lax.dynamic_index_in_dim(decay_chunks, index, keepdims=False)[:, None, None] * got
            + lax.dynamic_index_in_dim(end_chunks, index, keepdims=False)
        )
        pairs = [
            (src, src + 1)
            for src in range(max(0, step - CHUNKS + 1), min(step, n_ctx - 2) + 1)
        ]
        got = lax.ppermute(sent, "ctx", pairs)
        received.append(got)
    received = jnp.stack(received)
    prefix = lax.dynamic_slice_in_dim(received, jnp.maximum(ctx_pos - 1, 0), CHUNKS, 0)
    prefix = jnp.where(at_start, 0.0, prefix.reshape(local_heads, P_SIZE, N))

    all_decay = lax.all_gather(own_decay, "ctx")
    earlier = (lax.iota(jnp.int32, n_ctx) < ctx_pos)[:, None]
    decay_before = jnp.prod(jnp.where(earlier, all_decay, 1.0), axis=0)
    start_state = prefix + decay_before[:, None, None] * first_state
    end_state = own_decay[:, None, None] * start_state + local_end

    outs = []
    for blk in range(blocks):
        outs.append(
            block_output(
                starts[blk], x_view[blk], b_view[blk], c_view[blk], step_view[blk],
                cum_view[blk], skip_gain,
            )
        )
    local_out = jnp.concatenate(outs, axis=0)

    cum_dev = jnp.cumsum(log_decay, axis=1)
    readout = bc_conv[:, span:].reshape(tokens, local_groups, N)
    start_view = start_state.reshape(local_groups, local_heads // local_groups, P_SIZE, N)
    carried = jnp.einsum(
        "tgn,gjpn->tgjp", readout.astype(jnp.float32), start_view, precision=HIGHEST
    )
    carried = carried.reshape(tokens, local_heads, P_SIZE) * jnp.exp(-cum_dev).T[:, :, None]
    mixed = local_out + carried
    gate_act = jax.nn.silu(z_in[0].astype(jnp.float32)).reshape(tokens, local_heads, P_SIZE)
    gated = (
        (mixed * gate_act * live_mask[:, None, None])
        .reshape(1, tokens, local_heads * P_SIZE)
        .astype(jnp.bfloat16)
    )
    return (gated, end_state[None, None])


def solution(mesh):
    return jax.shard_map(
        on_device,
        mesh=mesh,
        in_specs=(
            P("req", "ctx", "head"),
            P("req", "ctx", None),
            P("req", "ctx", "head"),
            P("req", "head", "ctx"),
            P("head"),
            P("head"),
            P("head"),
            P(None, "head"),
            P(),
            P(("ctx", "req"), "head", None, None),
            P(("ctx", "req"), None, "head"),
            P("req", None, None),
            P(None, "head"),
            P(),
        ),
        out_specs=(P("req", "ctx", "head"), P("req", "ctx", "head", None, None)),
        check_vma=False,
    )
```

```python
from functools import partial

import jax
import jax.numpy as jnp
from jax import lax
from jax.sharding import PartitionSpec as P

H = 256
P_SIZE = 64
N = 256
G = 8
K = 4
STRETCH = 256
CHUNKS = 4


HIGHEST = lax.Precision.HIGHEST


def passed_along(value, axis, steps):
    count = lax.axis_size(axis)
    initial, last = (max(0, -steps), min(count, count - steps))
    return lax.ppermute(value, axis, [(source, source + steps) for source in range(initial, last)])


def causal_conv(prev_rows, rows, taps):
    padded = jnp.concatenate([prev_rows, rows.astype(jnp.float32)], axis=0)
    count = rows.shape[0]
    total = taps[0] * padded[0:count]
    for offset in range(1, taps.shape[0]):
        total = total + taps[offset] * padded[offset : offset + count]
    return jax.nn.silu(total).astype(jnp.bfloat16)


def block_state(running, x_blk, b_blk, step_blk, cum):
    block_len, head_count = x_blk.shape[0], x_blk.shape[1]
    group_count = b_blk.shape[1]
    per_group = head_count // group_count
    block_end = cum[:, -1:]
    factor = step_blk * jnp.exp(-(block_end - cum))
    weighted = (x_blk.astype(jnp.float32) * factor.T[:, :, None]).astype(jnp.bfloat16)
    weighted_view = weighted.reshape(block_len, group_count, per_group, running.shape[1])
    contrib = jnp.einsum(
        "qgjp,qgn->gjpn", weighted_view, b_blk, preferred_element_type=jnp.float32
    ).reshape(running.shape)
    return jnp.exp(-cum[:, -1])[:, None, None] * running + contrib


def block_output(running, x_blk, b_blk, c_blk, step_blk, cum, skip_gain):
    block_len = x_blk.shape[0]
    head_count = x_blk.shape[1]
    scores = jnp.einsum("qgn,sgn->gqs", c_blk, b_blk, preferred_element_type=jnp.float32)
    group_count = scores.shape[0]
    per_group = head_count // group_count
    scores_h = jnp.broadcast_to(
        scores[:, None], (group_count, per_group, block_len, block_len)
    ).reshape(head_count, block_len, block_len)
    row_ids = lax.broadcasted_iota(jnp.int32, (block_len, block_len), 0)
    col_ids = lax.broadcasted_iota(jnp.int32, (block_len, block_len), 1)
    causal = (row_ids >= col_ids)[None]
    decay_gap = jnp.where(causal, cum[:, :, None] - cum[:, None, :], 0.0)
    decay_mask = jnp.where(causal, jnp.exp(-decay_gap), 0.0)
    weights = (scores_h * decay_mask * step_blk[:, None, :]).astype(jnp.bfloat16)
    y_intra = jnp.einsum("hqs,shp->qhp", weights, x_blk, preferred_element_type=jnp.float32)
    state_view = running.reshape(group_count, per_group, running.shape[1], running.shape[2])
    y_state = jnp.einsum("qgn,gjpn->qgjp", c_blk.astype(jnp.float32), state_view, precision=HIGHEST)
    y_state = y_state.reshape(block_len, head_count, running.shape[1]) * jnp.exp(-cum).T[:, :, None]
    return y_intra + y_state + skip_gain[None, :, None] * x_blk.astype(jnp.float32)


def on_device(
    x_in,
    bc_in,
    z_in,
    dt_raw,
    dt_bias,
    decay_rate,
    skip_gain,
    conv_x,
    conv_bc,
    ssm_pool,
    conv_pool,
    bc_cache,
    owner,
    lengths,
):
    n_ctx = lax.axis_size("ctx")
    n_req = lax.axis_size("req")
    ctx_pos = lax.axis_index("ctx")
    head_pos = lax.axis_index("head")
    req_pos = lax.axis_index("req")
    local_heads = dt_raw.shape[1]
    tokens = x_in.shape[1]
    at_start = ctx_pos == 0

    want = owner[req_pos, 0]
    on_chip = (want // n_req) == ctx_pos
    mine = (want % n_req) == req_pos
    swap = [(src, n_req - 1 - src) for src in range(n_req)]
    other_pool, other_conv = lax.ppermute((ssm_pool[0], conv_pool[0]), "req", swap)
    state_pick = jnp.where(on_chip, jnp.where(mine, ssm_pool[0], other_pool), 0.0)
    conv_pick = jnp.where(on_chip, jnp.where(mine, conv_pool[0], other_conv), 0.0)
    picked = jnp.concatenate([state_pick.reshape(-1), conv_pick.reshape(-1)])
    picked, x_in, bc_in, dt_raw = lax.optimization_barrier((picked, x_in, bc_in, dt_raw))
    picked = lax.psum(picked, "ctx")
    first_state = picked[: state_pick.size].reshape(state_pick.shape)
    first_conv = picked[state_pick.size :].reshape(conv_pick.shape)

    tail_x = x_in[0, tokens - (K - 1) :, :]
    tail_bc = bc_in[0, tokens - (K - 1) :, :]
    prev_x, prev_bc = passed_along((tail_x, tail_bc), "ctx", 1)
    prev_x = jnp.where(at_start, first_conv, prev_x.astype(jnp.float32))
    prev_bc = jnp.where(at_start, bc_cache[0], prev_bc.astype(jnp.float32))
    per_group = H // G
    local_groups = max(1, local_heads // per_group)
    group_start = head_pos * local_heads // per_group
    span = local_groups * N

    def pick_groups(values):
        input_cols = lax.dynamic_slice_in_dim(values, group_start * N, span, 1)
        output_cols = lax.dynamic_slice_in_dim(values, G * N + group_start * N, span, 1)
        return jnp.concatenate([input_cols, output_cols], axis=1)

    x_head = causal_conv(prev_x, x_in[0, : K - 1], conv_x)
    x_rest = causal_conv(x_in[0, : K - 1].astype(jnp.float32), x_in[0, K - 1 :], conv_x)
    x_conv = jnp.concatenate([x_head, x_rest], axis=0)
    bc_conv = causal_conv(pick_groups(prev_bc), pick_groups(bc_in[0]), pick_groups(conv_bc))
    positions = ctx_pos * tokens + lax.iota(jnp.int32, tokens)
    live_mask = (positions < lengths[req_pos]).astype(jnp.float32)
    step_size = jax.nn.softplus(dt_raw[0] + dt_bias[:, None]) * live_mask[None, :]
    log_decay = step_size * decay_rate[:, None]
    blocks = tokens // STRETCH
    x_view = x_conv.reshape(blocks, STRETCH, local_heads, P_SIZE)
    b_view = bc_conv[:, :span].reshape(blocks, STRETCH, local_groups, N)
    c_view = bc_conv[:, span:].reshape(blocks, STRETCH, local_groups, N)
    step_view = step_size.reshape(local_heads, blocks, STRETCH).transpose(1, 0, 2)
    log_view = log_decay.reshape(local_heads, blocks, STRETCH).transpose(1, 0, 2)
    cum_view = jnp.cumsum(log_view, axis=2)

    running = jnp.zeros((local_heads, P_SIZE, N), jnp.float32)
    starts = []
    for blk in range(blocks):
        starts.append(running)
        running = block_state(running, x_view[blk], b_view[blk], step_view[blk], cum_view[blk])
    local_end = running
    own_decay = jnp.exp(-jnp.sum(log_decay, axis=1))

    chunk = local_heads // CHUNKS
    end_chunks = local_end.reshape(CHUNKS, chunk, P_SIZE, N)
    init_chunks = first_state.reshape(CHUNKS, chunk, P_SIZE, N)
    decay_chunks = own_decay.reshape(CHUNKS, chunk)
    got = jnp.zeros((chunk, P_SIZE, N), jnp.float32)
    received = []
    for step in range(n_ctx + CHUNKS - 2):
        index = jnp.clip(step - ctx_pos, 0, CHUNKS - 1)
        prior = jnp.where(
            at_start, lax.dynamic_index_in_dim(init_chunks, index, keepdims=False), got
        )
        sent = (
            lax.dynamic_index_in_dim(decay_chunks, index, keepdims=False)[:, None, None] * prior
            + lax.dynamic_index_in_dim(end_chunks, index, keepdims=False)
        )
        pairs = [
            (src, src + 1)
            for src in range(max(0, step - CHUNKS + 1), min(step, n_ctx - 2) + 1)
        ]
        got = lax.ppermute(sent, "ctx", pairs)
        received.append(got)
    received = jnp.stack(received)
    prefix = lax.dynamic_slice_in_dim(received, jnp.maximum(ctx_pos - 1, 0), CHUNKS, 0)
    start_state = jnp.where(at_start, first_state, prefix.reshape(local_heads, P_SIZE, N))
    end_state = own_decay[:, None, None] * start_state + local_end

    outs = []
    for blk in range(blocks):
        outs.append(
            block_output(
                starts[blk], x_view[blk], b_view[blk], c_view[blk], step_view[blk],
                cum_view[blk], skip_gain,
            )
        )
    local_out = jnp.concatenate(outs, axis=0)

    cum_dev = jnp.cumsum(log_decay, axis=1)
    readout = bc_conv[:, span:].reshape(tokens, local_groups, N)
    start_view = start_state.reshape(local_groups, local_heads // local_groups, P_SIZE, N)
    carried = jnp.einsum(
        "tgn,gjpn->tgjp", readout.astype(jnp.float32), start_view, precision=HIGHEST
    )
    carried = carried.reshape(tokens, local_heads, P_SIZE) * jnp.exp(-cum_dev).T[:, :, None]
    mixed = local_out + carried
    gate_act = jax.nn.silu(z_in[0].astype(jnp.float32)).reshape(tokens, local_heads, P_SIZE)
    gated = (
        (mixed * gate_act * live_mask[:, None, None])
        .reshape(1, tokens, local_heads * P_SIZE)
        .astype(jnp.bfloat16)
    )
    return (gated, end_state[None, None])


def solution(mesh):
    return jax.shard_map(
        on_device,
        mesh=mesh,
        in_specs=(
            P("req", "ctx", "head"),
            P("req", "ctx", None),
            P("req", "ctx", "head"),
            P("req", "head", "ctx"),
            P("head"),
            P("head"),
            P("head"),
            P(None, "head"),
            P(),
            P(("ctx", "req"), "head", None, None),
            P(("ctx", "req"), None, "head"),
            P("req", None, None),
            P(None, "head"),
            P(),
        ),
        out_specs=(P("req", "ctx", "head"), P("req", "ctx", "head", None, None)),
        check_vma=False,
    )
```

```python
from functools import partial

import jax
import jax.numpy as jnp
from jax import lax
from jax.sharding import PartitionSpec as P

H = 256
P_SIZE = 64
N = 256
G = 8
K = 4
STRETCH = 256
CHUNKS = 4


HIGHEST = lax.Precision.HIGHEST


def passed_along(value, axis, steps):
    count = lax.axis_size(axis)
    initial, last = (max(0, -steps), min(count, count - steps))
    return lax.ppermute(value, axis, [(source, source + steps) for source in range(initial, last)])


def causal_conv(prev_rows, rows, taps):
    padded = jnp.concatenate([prev_rows, rows.astype(jnp.float32)], axis=0)
    count = rows.shape[0]
    total = taps[0] * padded[0:count]
    for offset in range(1, taps.shape[0]):
        total = total + taps[offset] * padded[offset : offset + count]
    return jax.nn.silu(total).astype(jnp.bfloat16)


def block_state(running, x_blk, b_blk, step_blk, cum):
    block_len, head_count = x_blk.shape[0], x_blk.shape[1]
    group_count = b_blk.shape[1]
    per_group = head_count // group_count
    block_end = cum[:, -1:]
    factor = step_blk * jnp.exp(-(block_end - cum))
    weighted = (x_blk.astype(jnp.float32) * factor.T[:, :, None]).astype(jnp.bfloat16)
    weighted_view = weighted.reshape(block_len, group_count, per_group, running.shape[1])
    contrib = jnp.einsum(
        "qgjp,qgn->gjpn", weighted_view, b_blk, preferred_element_type=jnp.float32
    ).reshape(running.shape)
    return jnp.exp(-cum[:, -1])[:, None, None] * running + contrib


def block_intra(x_blk, b_blk, c_blk, step_blk, cum, skip_gain):
    block_len = x_blk.shape[0]
    head_count = x_blk.shape[1]
    scores = jnp.einsum("qgn,sgn->gqs", c_blk, b_blk, preferred_element_type=jnp.float32)
    group_count = scores.shape[0]
    per_group = head_count // group_count
    scores_h = jnp.broadcast_to(
        scores[:, None], (group_count, per_group, block_len, block_len)
    ).reshape(head_count, block_len, block_len)
    row_ids = lax.broadcasted_iota(jnp.int32, (block_len, block_len), 0)
    col_ids = lax.broadcasted_iota(jnp.int32, (block_len, block_len), 1)
    causal = (row_ids >= col_ids)[None]
    decay_gap = jnp.where(causal, cum[:, :, None] - cum[:, None, :], 0.0)
    decay_mask = jnp.where(causal, jnp.exp(-decay_gap), 0.0)
    weights = (scores_h * decay_mask * step_blk[:, None, :]).astype(jnp.bfloat16)
    y_intra = jnp.einsum("hqs,shp->qhp", weights, x_blk, preferred_element_type=jnp.float32)
    return y_intra, skip_gain[None, :, None] * x_blk.astype(jnp.float32)


def block_from_state(running, c_blk, cum):
    block_len = c_blk.shape[0]
    group_count = c_blk.shape[1]
    head_count = running.shape[0]
    per_group = head_count // group_count
    state_view = running.reshape(group_count, per_group, running.shape[1], running.shape[2])
    y_state = jnp.einsum("qgn,gjpn->qgjp", c_blk.astype(jnp.float32), state_view, precision=HIGHEST)
    return y_state.reshape(block_len, head_count, running.shape[1]) * jnp.exp(-cum).T[:, :, None]


def on_device(
    x_in,
    bc_in,
    z_in,
    dt_raw,
    dt_bias,
    decay_rate,
    skip_gain,
    conv_x,
    conv_bc,
    ssm_pool,
    conv_pool,
    bc_cache,
    owner,
    lengths,
):
    n_ctx = lax.axis_size("ctx")
    n_req = lax.axis_size("req")
    ctx_pos = lax.axis_index("ctx")
    head_pos = lax.axis_index("head")
    req_pos = lax.axis_index("req")
    local_heads = dt_raw.shape[1]
    tokens = x_in.shape[1]
    at_start = ctx_pos == 0

    want = owner[req_pos, 0]
    on_chip = (want // n_req) == ctx_pos
    mine = (want % n_req) == req_pos
    swap = [(src, n_req - 1 - src) for src in range(n_req)]
    other_pool, other_conv = lax.ppermute((ssm_pool[0], conv_pool[0]), "req", swap)
    state_pick = jnp.where(on_chip, jnp.where(mine, ssm_pool[0], other_pool), 0.0)
    conv_pick = jnp.where(on_chip, jnp.where(mine, conv_pool[0], other_conv), 0.0)
    picked = jnp.concatenate([state_pick.reshape(-1), conv_pick.reshape(-1)])
    picked, x_in, bc_in, z_in, dt_raw = lax.optimization_barrier(
        (picked, x_in, bc_in, z_in, dt_raw)
    )
    picked = lax.psum(picked, "ctx")
    first_state = picked[: state_pick.size].reshape(state_pick.shape)
    first_conv = picked[state_pick.size :].reshape(conv_pick.shape)

    tail_x = x_in[0, tokens - (K - 1) :, :]
    tail_bc = bc_in[0, tokens - (K - 1) :, :]
    prev_x, prev_bc = passed_along((tail_x, tail_bc), "ctx", 1)
    prev_x = jnp.where(at_start, first_conv, prev_x.astype(jnp.float32))
    prev_bc = jnp.where(at_start, bc_cache[0], prev_bc.astype(jnp.float32))
    per_group = H // G
    local_groups = max(1, local_heads // per_group)
    group_start = head_pos * local_heads // per_group
    span = local_groups * N

    def pick_groups(values):
        input_cols = lax.dynamic_slice_in_dim(values, group_start * N, span, 1)
        output_cols = lax.dynamic_slice_in_dim(values, G * N + group_start * N, span, 1)
        return jnp.concatenate([input_cols, output_cols], axis=1)

    x_head = causal_conv(prev_x, x_in[0, : K - 1], conv_x)
    x_rest = causal_conv(x_in[0, : K - 1].astype(jnp.float32), x_in[0, K - 1 :], conv_x)
    x_conv = jnp.concatenate([x_head, x_rest], axis=0)
    bc_conv = causal_conv(pick_groups(prev_bc), pick_groups(bc_in[0]), pick_groups(conv_bc))
    positions = ctx_pos * tokens + lax.iota(jnp.int32, tokens)
    live_mask = (positions < lengths[req_pos]).astype(jnp.float32)
    step_size = jax.nn.softplus(dt_raw[0] + dt_bias[:, None]) * live_mask[None, :]
    log_decay = step_size * decay_rate[:, None]
    blocks = tokens // STRETCH
    x_view = x_conv.reshape(blocks, STRETCH, local_heads, P_SIZE)
    b_view = bc_conv[:, :span].reshape(blocks, STRETCH, local_groups, N)
    c_view = bc_conv[:, span:].reshape(blocks, STRETCH, local_groups, N)
    step_view = step_size.reshape(local_heads, blocks, STRETCH).transpose(1, 0, 2)
    log_view = log_decay.reshape(local_heads, blocks, STRETCH).transpose(1, 0, 2)
    cum_view = jnp.cumsum(log_view, axis=2)

    running = jnp.zeros((local_heads, P_SIZE, N), jnp.float32)
    starts = []
    for blk in range(blocks):
        starts.append(running)
        running = block_state(running, x_view[blk], b_view[blk], step_view[blk], cum_view[blk])
    local_end = running
    own_decay = jnp.exp(-jnp.sum(log_decay, axis=1))

    intra = [
        block_intra(x_view[blk], b_view[blk], c_view[blk], step_view[blk], cum_view[blk], skip_gain)
        for blk in range(blocks)
    ]
    first_state, later_intra = lax.optimization_barrier((first_state, intra[1:]))
    intra = intra[:1] + list(later_intra)

    chunk = local_heads // CHUNKS
    end_chunks = local_end.reshape(CHUNKS, chunk, P_SIZE, N)
    init_chunks = first_state.reshape(CHUNKS, chunk, P_SIZE, N)
    decay_chunks = own_decay.reshape(CHUNKS, chunk)
    got = jnp.zeros((chunk, P_SIZE, N), jnp.float32)
    received = []
    for step in range(n_ctx + CHUNKS - 2):
        index = jnp.clip(step - ctx_pos, 0, CHUNKS - 1)
        prior = jnp.where(
            at_start, lax.dynamic_index_in_dim(init_chunks, index, keepdims=False), got
        )
        sent = (
            lax.dynamic_index_in_dim(decay_chunks, index, keepdims=False)[:, None, None] * prior
            + lax.dynamic_index_in_dim(end_chunks, index, keepdims=False)
        )
        pairs = [
            (src, src + 1)
            for src in range(max(0, step - CHUNKS + 1), min(step, n_ctx - 2) + 1)
        ]
        got = lax.ppermute(sent, "ctx", pairs)
        received.append(got)
    received = jnp.stack(received)
    prefix = lax.dynamic_slice_in_dim(received, jnp.maximum(ctx_pos - 1, 0), CHUNKS, 0)
    start_state = jnp.where(at_start, first_state, prefix.reshape(local_heads, P_SIZE, N))
    end_state = own_decay[:, None, None] * start_state + local_end

    outs = []
    for blk in range(blocks):
        y_intra, y_skip = intra[blk]
        outs.append(y_intra + block_from_state(starts[blk], c_view[blk], cum_view[blk]) + y_skip)
    local_out = jnp.concatenate(outs, axis=0)

    cum_dev = jnp.cumsum(log_decay, axis=1)
    readout = bc_conv[:, span:].reshape(tokens, local_groups, N)
    start_view = start_state.reshape(local_groups, local_heads // local_groups, P_SIZE, N)
    carried = jnp.einsum(
        "tgn,gjpn->tgjp", readout.astype(jnp.float32), start_view, precision=HIGHEST
    )
    carried = carried.reshape(tokens, local_heads, P_SIZE) * jnp.exp(-cum_dev).T[:, :, None]
    mixed = local_out + carried
    gate_act = jax.nn.silu(z_in[0].astype(jnp.float32)).reshape(tokens, local_heads, P_SIZE)
    gated = (
        (mixed * gate_act * live_mask[:, None, None])
        .reshape(1, tokens, local_heads * P_SIZE)
        .astype(jnp.bfloat16)
    )
    return (gated, end_state[None, None])


def solution(mesh):
    return jax.shard_map(
        on_device,
        mesh=mesh,
        in_specs=(
            P("req", "ctx", "head"),
            P("req", "ctx", None),
            P("req", "ctx", "head"),
            P("req", "head", "ctx"),
            P("head"),
            P("head"),
            P("head"),
            P(None, "head"),
            P(),
            P(("ctx", "req"), "head", None, None),
            P(("ctx", "req"), None, "head"),
            P("req", None, None),
            P(None, "head"),
            P(),
        ),
        out_specs=(P("req", "ctx", "head"), P("req", "ctx", "head", None, None)),
        check_vma=False,
    )
```

```python
from functools import partial

import jax
import jax.numpy as jnp
from jax import lax
from jax.sharding import PartitionSpec as P

H = 256
P_SIZE = 64
N = 256
G = 8
K = 4
STRETCH = 256
CHUNKS = 4


HIGHEST = lax.Precision.HIGHEST


def passed_along(value, axis, steps):
    count = lax.axis_size(axis)
    initial, last = (max(0, -steps), min(count, count - steps))
    return lax.ppermute(value, axis, [(source, source + steps) for source in range(initial, last)])


def causal_conv(prev_rows, rows, taps):
    padded = jnp.concatenate([prev_rows, rows.astype(jnp.float32)], axis=0)
    count = rows.shape[0]
    total = taps[0] * padded[0:count]
    for offset in range(1, taps.shape[0]):
        total = total + taps[offset] * padded[offset : offset + count]
    return jax.nn.silu(total).astype(jnp.bfloat16)


def block_state(running, x_blk, b_blk, step_blk, cum):
    block_len, head_count = x_blk.shape[0], x_blk.shape[1]
    group_count = b_blk.shape[1]
    per_group = head_count // group_count
    block_end = cum[:, -1:]
    factor = step_blk * jnp.exp(-(block_end - cum))
    weighted = (x_blk.astype(jnp.float32) * factor.T[:, :, None]).astype(jnp.bfloat16)
    weighted_view = weighted.reshape(block_len, group_count, per_group, running.shape[1])
    contrib = jnp.einsum(
        "qgjp,qgn->gjpn", weighted_view, b_blk, preferred_element_type=jnp.float32
    ).reshape(running.shape)
    return jnp.exp(-cum[:, -1])[:, None, None] * running + contrib


def block_intra(x_blk, b_blk, c_blk, step_blk, cum, skip_gain):
    block_len = x_blk.shape[0]
    head_count = x_blk.shape[1]
    scores = jnp.einsum("qgn,sgn->gqs", c_blk, b_blk, preferred_element_type=jnp.float32)
    group_count = scores.shape[0]
    per_group = head_count // group_count
    scores_h = jnp.broadcast_to(
        scores[:, None], (group_count, per_group, block_len, block_len)
    ).reshape(head_count, block_len, block_len)
    row_ids = lax.broadcasted_iota(jnp.int32, (block_len, block_len), 0)
    col_ids = lax.broadcasted_iota(jnp.int32, (block_len, block_len), 1)
    causal = (row_ids >= col_ids)[None]
    decay_gap = jnp.where(causal, cum[:, :, None] - cum[:, None, :], 0.0)
    decay_mask = jnp.where(causal, jnp.exp(-decay_gap), 0.0)
    weights = (scores_h * decay_mask * step_blk[:, None, :]).astype(jnp.bfloat16)
    y_intra = jnp.einsum("hqs,shp->qhp", weights, x_blk, preferred_element_type=jnp.float32)
    return y_intra, skip_gain[None, :, None] * x_blk.astype(jnp.float32)


def block_from_state(running, c_blk, cum):
    block_len = c_blk.shape[0]
    group_count = c_blk.shape[1]
    head_count = running.shape[0]
    per_group = head_count // group_count
    state_view = running.reshape(group_count, per_group, running.shape[1], running.shape[2])
    y_state = jnp.einsum("qgn,gjpn->qgjp", c_blk.astype(jnp.float32), state_view, precision=HIGHEST)
    return y_state.reshape(block_len, head_count, running.shape[1]) * jnp.exp(-cum).T[:, :, None]


def on_device(
    x_in,
    bc_in,
    z_in,
    dt_raw,
    dt_bias,
    decay_rate,
    skip_gain,
    conv_x,
    conv_bc,
    ssm_pool,
    conv_pool,
    bc_cache,
    owner,
    lengths,
):
    n_ctx = lax.axis_size("ctx")
    n_req = lax.axis_size("req")
    ctx_pos = lax.axis_index("ctx")
    head_pos = lax.axis_index("head")
    req_pos = lax.axis_index("req")
    local_heads = dt_raw.shape[1]
    tokens = x_in.shape[1]
    at_start = ctx_pos == 0

    want = owner[req_pos, 0]
    on_chip = (want // n_req) == ctx_pos
    mine = (want % n_req) == req_pos
    swap = [(src, n_req - 1 - src) for src in range(n_req)]
    other_pool, other_conv = lax.ppermute((ssm_pool[0], conv_pool[0]), "req", swap)
    state_pick = jnp.where(on_chip, jnp.where(mine, ssm_pool[0], other_pool), 0.0)
    conv_pick = jnp.where(on_chip, jnp.where(mine, conv_pool[0], other_conv), 0.0)
    picked = jnp.concatenate([state_pick.reshape(-1), conv_pick.reshape(-1)])
    picked, x_in, bc_in, z_in, dt_raw = lax.optimization_barrier(
        (picked, x_in, bc_in, z_in, dt_raw)
    )
    picked = lax.psum(picked, "ctx")
    first_state = picked[: state_pick.size].reshape(state_pick.shape)
    first_conv = picked[state_pick.size :].reshape(conv_pick.shape)

    tail_x = x_in[0, tokens - (K - 1) :, :]
    tail_bc = bc_in[0, tokens - (K - 1) :, :]
    prev_x, prev_bc = passed_along((tail_x, tail_bc), "ctx", 1)
    prev_x = jnp.where(at_start, first_conv, prev_x.astype(jnp.float32))
    prev_bc = jnp.where(at_start, bc_cache[0], prev_bc.astype(jnp.float32))
    per_group = H // G
    local_groups = max(1, local_heads // per_group)
    group_start = head_pos * local_heads // per_group
    span = local_groups * N

    def pick_groups(values):
        input_cols = lax.dynamic_slice_in_dim(values, group_start * N, span, 1)
        output_cols = lax.dynamic_slice_in_dim(values, G * N + group_start * N, span, 1)
        return jnp.concatenate([input_cols, output_cols], axis=1)

    x_head = causal_conv(prev_x, x_in[0, : K - 1], conv_x)
    x_rest = causal_conv(x_in[0, : K - 1].astype(jnp.float32), x_in[0, K - 1 :], conv_x)
    x_conv = jnp.concatenate([x_head, x_rest], axis=0)
    bc_conv = causal_conv(pick_groups(prev_bc), pick_groups(bc_in[0]), pick_groups(conv_bc))
    positions = ctx_pos * tokens + lax.iota(jnp.int32, tokens)
    live_mask = (positions < lengths[req_pos]).astype(jnp.float32)
    step_size = jax.nn.softplus(dt_raw[0] + dt_bias[:, None]) * live_mask[None, :]
    log_decay = step_size * decay_rate[:, None]
    blocks = tokens // STRETCH
    x_view = x_conv.reshape(blocks, STRETCH, local_heads, P_SIZE)
    b_view = bc_conv[:, :span].reshape(blocks, STRETCH, local_groups, N)
    c_view = bc_conv[:, span:].reshape(blocks, STRETCH, local_groups, N)
    step_view = step_size.reshape(local_heads, blocks, STRETCH).transpose(1, 0, 2)
    log_view = log_decay.reshape(local_heads, blocks, STRETCH).transpose(1, 0, 2)
    cum_view = jnp.cumsum(log_view, axis=2)

    running = jnp.zeros((local_heads, P_SIZE, N), jnp.float32)
    starts = []
    for blk in range(blocks):
        starts.append(running)
        running = block_state(running, x_view[blk], b_view[blk], step_view[blk], cum_view[blk])
    local_end = running
    own_decay = jnp.exp(-jnp.sum(log_decay, axis=1))

    intra = [
        block_intra(x_view[blk], b_view[blk], c_view[blk], step_view[blk], cum_view[blk], skip_gain)
        for blk in range(blocks)
    ]
    first_state, later_intra = lax.optimization_barrier((first_state, intra[1:]))
    intra = intra[:1] + list(later_intra)

    chunk = local_heads // CHUNKS
    end_chunks = local_end.reshape(CHUNKS, chunk, P_SIZE, N)
    init_chunks = first_state.reshape(CHUNKS, chunk, P_SIZE, N)
    decay_chunks = own_decay.reshape(CHUNKS, chunk)
    got = jnp.zeros((chunk, P_SIZE, N), jnp.float32)
    received = []
    for step in range(n_ctx + CHUNKS - 2):
        index = jnp.clip(step - ctx_pos, 0, CHUNKS - 1)
        prior = jnp.where(
            at_start, lax.dynamic_index_in_dim(init_chunks, index, keepdims=False), got
        )
        sent = (
            lax.dynamic_index_in_dim(decay_chunks, index, keepdims=False)[:, None, None] * prior
            + lax.dynamic_index_in_dim(end_chunks, index, keepdims=False)
        )
        pairs = [
            (src, src + 1)
            for src in range(max(0, step - CHUNKS + 1), min(step, n_ctx - 2) + 1)
        ]
        got = lax.ppermute(sent.astype(jnp.bfloat16), "ctx", pairs).astype(jnp.float32)
        received.append(got)
    received = jnp.stack(received)
    prefix = lax.dynamic_slice_in_dim(received, jnp.maximum(ctx_pos - 1, 0), CHUNKS, 0)
    start_state = jnp.where(at_start, first_state, prefix.reshape(local_heads, P_SIZE, N))
    end_state = own_decay[:, None, None] * start_state + local_end

    outs = []
    for blk in range(blocks):
        y_intra, y_skip = intra[blk]
        outs.append(y_intra + block_from_state(starts[blk], c_view[blk], cum_view[blk]) + y_skip)
    local_out = jnp.concatenate(outs, axis=0)

    cum_dev = jnp.cumsum(log_decay, axis=1)
    readout = bc_conv[:, span:].reshape(tokens, local_groups, N)
    start_view = start_state.reshape(local_groups, local_heads // local_groups, P_SIZE, N)
    carried = jnp.einsum(
        "tgn,gjpn->tgjp", readout.astype(jnp.float32), start_view, precision=HIGHEST
    )
    carried = carried.reshape(tokens, local_heads, P_SIZE) * jnp.exp(-cum_dev).T[:, :, None]
    mixed = local_out + carried
    gate_act = jax.nn.silu(z_in[0].astype(jnp.float32)).reshape(tokens, local_heads, P_SIZE)
    gated = (
        (mixed * gate_act * live_mask[:, None, None])
        .reshape(1, tokens, local_heads * P_SIZE)
        .astype(jnp.bfloat16)
    )
    return (gated, end_state[None, None])


def solution(mesh):
    return jax.shard_map(
        on_device,
        mesh=mesh,
        in_specs=(
            P("req", "ctx", "head"),
            P("req", "ctx", None),
            P("req", "ctx", "head"),
            P("req", "head", "ctx"),
            P("head"),
            P("head"),
            P("head"),
            P(None, "head"),
            P(),
            P(("ctx", "req"), "head", None, None),
            P(("ctx", "req"), None, "head"),
            P("req", None, None),
            P(None, "head"),
            P(),
        ),
        out_specs=(P("req", "ctx", "head"), P("req", "ctx", "head", None, None)),
        check_vma=False,
    )
```

```python
import jax
import jax.numpy as jnp
from jax import lax
from jax.sharding import PartitionSpec as P


H = 256
P_SIZE = 64
N = 256
G = 8
K = 4
STRETCH = 256
CHUNKS = 4


HIGHEST = lax.Precision.HIGHEST


def passed_along(value, axis, steps):
    count = lax.axis_size(axis)
    initial, last = (max(0, -steps), min(count, count - steps))
    return lax.ppermute(value, axis, [(source, source + steps) for source in range(initial, last)])


def causal_conv(prev_rows, rows, taps):
    padded = jnp.concatenate([prev_rows, rows.astype(jnp.float32)], axis=0)
    count = rows.shape[0]
    total = taps[0] * padded[0:count]
    for offset in range(1, taps.shape[0]):
        total = total + taps[offset] * padded[offset : offset + count]
    return jax.nn.silu(total).astype(jnp.bfloat16)


def block_state(running, x_blk, b_blk, step_blk, cum):
    block_len, head_count = x_blk.shape[0], x_blk.shape[1]
    group_count = b_blk.shape[1]
    per_group = head_count // group_count
    block_end = cum[:, -1:]
    factor = step_blk * jnp.exp(-(block_end - cum))
    weighted = (x_blk.astype(jnp.float32) * factor.T[:, :, None]).astype(jnp.bfloat16)
    weighted_view = weighted.reshape(block_len, group_count, per_group, running.shape[1])
    contrib = jnp.einsum(
        "qgjp,qgn->gjpn", weighted_view, b_blk, preferred_element_type=jnp.float32
    ).reshape(running.shape)
    return jnp.exp(-cum[:, -1])[:, None, None] * running + contrib


def block_intra(x_blk, b_blk, c_blk, step_blk, cum, skip_gain):
    block_len = x_blk.shape[0]
    head_count = x_blk.shape[1]
    scores = jnp.einsum("qgn,sgn->gqs", c_blk, b_blk, preferred_element_type=jnp.float32)
    group_count = scores.shape[0]
    per_group = head_count // group_count
    scores_h = jnp.broadcast_to(
        scores[:, None], (group_count, per_group, block_len, block_len)
    ).reshape(head_count, block_len, block_len)
    row_ids = lax.broadcasted_iota(jnp.int32, (block_len, block_len), 0)
    col_ids = lax.broadcasted_iota(jnp.int32, (block_len, block_len), 1)
    causal = (row_ids >= col_ids)[None]
    decay_gap = jnp.where(causal, cum[:, :, None] - cum[:, None, :], 0.0)
    decay_mask = jnp.where(causal, jnp.exp(-decay_gap), 0.0)
    weights = (scores_h * decay_mask * step_blk[:, None, :]).astype(jnp.bfloat16)
    y_intra = jnp.einsum("hqs,shp->qhp", weights, x_blk, preferred_element_type=jnp.float32)
    return y_intra, skip_gain[None, :, None] * x_blk.astype(jnp.float32)


def block_from_state(running, c_blk, cum):
    block_len = c_blk.shape[0]
    group_count = c_blk.shape[1]
    head_count = running.shape[0]
    per_group = head_count // group_count
    state_view = running.reshape(group_count, per_group, running.shape[1], running.shape[2])
    y_state = jnp.einsum("qgn,gjpn->qgjp", c_blk.astype(jnp.float32), state_view, precision=HIGHEST)
    return y_state.reshape(block_len, head_count, running.shape[1]) * jnp.exp(-cum).T[:, :, None]


def device_body(
    x_in,
    bc_in,
    z_in,
    dt_raw,
    dt_bias,
    decay_rate,
    skip_gain,
    conv_x,
    conv_bc,
    ssm_pool,
    conv_pool,
    bc_cache,
    owner,
    lengths,
):
    n_ctx = lax.axis_size("ctx")
    n_req = lax.axis_size("req")
    ctx_pos = lax.axis_index("ctx")
    head_pos = lax.axis_index("head")
    req_pos = lax.axis_index("req")
    local_heads = dt_raw.shape[1]
    tokens = x_in.shape[1]
    at_start = ctx_pos == 0

    want = owner[req_pos, 0]
    on_chip = (want // n_req) == ctx_pos
    mine = (want % n_req) == req_pos
    swap = [(src, n_req - 1 - src) for src in range(n_req)]
    other_pool, other_conv = lax.ppermute((ssm_pool[0], conv_pool[0]), "req", swap)
    state_pick = jnp.where(on_chip, jnp.where(mine, ssm_pool[0], other_pool), 0.0)
    conv_pick = jnp.where(on_chip, jnp.where(mine, conv_pool[0], other_conv), 0.0)
    half = state_pick.shape[0] // 2
    early = jnp.concatenate([state_pick[:half].reshape(-1), conv_pick.reshape(-1)])
    late = state_pick[half:]
    early, late, x_in, bc_in, z_in, dt_raw = lax.optimization_barrier(
        (early, late, x_in, bc_in, z_in, dt_raw)
    )
    early = lax.psum(early, "ctx")
    late = lax.psum_scatter(late, "ctx", scatter_dimension=1, tiled=True)
    late = lax.all_gather(late, "ctx", axis=1, tiled=True)
    first_conv = early[late.size :].reshape(conv_pick.shape)
    early_state = early[: late.size].reshape(late.shape)
    first_state = jnp.concatenate([early_state, late], axis=0)

    tail_x = x_in[0, tokens - (K - 1) :, :]
    tail_bc = bc_in[0, tokens - (K - 1) :, :]
    prev_x, prev_bc = passed_along((tail_x, tail_bc), "ctx", 1)
    prev_x = jnp.where(at_start, first_conv, prev_x.astype(jnp.float32))
    prev_bc = jnp.where(at_start, bc_cache[0], prev_bc.astype(jnp.float32))
    per_group = H // G
    local_groups = max(1, local_heads // per_group)
    group_start = head_pos * local_heads // per_group
    span = local_groups * N

    def pick_groups(values):
        input_cols = lax.dynamic_slice_in_dim(values, group_start * N, span, 1)
        output_cols = lax.dynamic_slice_in_dim(values, G * N + group_start * N, span, 1)
        return jnp.concatenate([input_cols, output_cols], axis=1)

    x_head = causal_conv(prev_x, x_in[0, : K - 1], conv_x)
    x_rest = causal_conv(x_in[0, : K - 1].astype(jnp.float32), x_in[0, K - 1 :], conv_x)
    x_conv = jnp.concatenate([x_head, x_rest], axis=0)
    bc_conv = causal_conv(pick_groups(prev_bc), pick_groups(bc_in[0]), pick_groups(conv_bc))
    positions = ctx_pos * tokens + lax.iota(jnp.int32, tokens)
    live_mask = (positions < lengths[req_pos]).astype(jnp.float32)
    step_size = jax.nn.softplus(dt_raw[0] + dt_bias[:, None]) * live_mask[None, :]
    log_decay = step_size * decay_rate[:, None]
    blocks = tokens // STRETCH
    x_view = x_conv.reshape(blocks, STRETCH, local_heads, P_SIZE)
    b_view = bc_conv[:, :span].reshape(blocks, STRETCH, local_groups, N)
    c_view = bc_conv[:, span:].reshape(blocks, STRETCH, local_groups, N)
    step_view = step_size.reshape(local_heads, blocks, STRETCH).transpose(1, 0, 2)
    log_view = log_decay.reshape(local_heads, blocks, STRETCH).transpose(1, 0, 2)
    cum_view = jnp.cumsum(log_view, axis=2)

    running = jnp.zeros((local_heads, P_SIZE, N), jnp.float32)
    starts = []
    for blk in range(blocks):
        starts.append(running)
        running = block_state(running, x_view[blk], b_view[blk], step_view[blk], cum_view[blk])
    local_end = running
    own_decay = jnp.exp(-jnp.sum(log_decay, axis=1))

    intra = [
        block_intra(x_view[blk], b_view[blk], c_view[blk], step_view[blk], cum_view[blk], skip_gain)
        for blk in range(blocks)
    ]
    first_state, later_intra = lax.optimization_barrier((first_state, intra[1:]))
    intra = intra[:1] + list(later_intra)

    chunk = local_heads // CHUNKS
    end_chunks = local_end.reshape(CHUNKS, chunk, P_SIZE, N)
    init_chunks = [
        piece.reshape(-1, chunk, P_SIZE, N)[part]
        for piece in (early_state, late)
        for part in range(CHUNKS // 2)
    ]
    decay_chunks = own_decay.reshape(CHUNKS, chunk)
    got = jnp.zeros((chunk, P_SIZE, N), jnp.float32)
    received = []
    for step in range(n_ctx + CHUNKS - 2):
        index = jnp.clip(step - ctx_pos, 0, CHUNKS - 1)
        prior = jnp.where(at_start, init_chunks[min(step, CHUNKS - 1)], got)
        sent = (
            lax.dynamic_index_in_dim(decay_chunks, index, keepdims=False)[:, None, None] * prior
            + lax.dynamic_index_in_dim(end_chunks, index, keepdims=False)
        )
        pairs = [
            (src, src + 1)
            for src in range(max(0, step - CHUNKS + 1), min(step, n_ctx - 2) + 1)
        ]
        got = lax.ppermute(sent.astype(jnp.bfloat16), "ctx", pairs).astype(jnp.float32)
        received.append(got)
    received = jnp.stack(received)
    prefix = lax.dynamic_slice_in_dim(received, jnp.maximum(ctx_pos - 1, 0), CHUNKS, 0)
    start_state = jnp.where(at_start, first_state, prefix.reshape(local_heads, P_SIZE, N))
    end_state = own_decay[:, None, None] * start_state + local_end

    outs = []
    for blk in range(blocks):
        y_intra, y_skip = intra[blk]
        outs.append(y_intra + block_from_state(starts[blk], c_view[blk], cum_view[blk]) + y_skip)
    local_out = jnp.concatenate(outs, axis=0)

    cum_dev = jnp.cumsum(log_decay, axis=1)
    readout = bc_conv[:, span:].reshape(tokens, local_groups, N)
    start_view = start_state.reshape(local_groups, local_heads // local_groups, P_SIZE, N)
    carried = jnp.einsum(
        "tgn,gjpn->tgjp", readout.astype(jnp.float32), start_view, precision=HIGHEST
    )
    carried = carried.reshape(tokens, local_heads, P_SIZE) * jnp.exp(-cum_dev).T[:, :, None]
    mixed = local_out + carried
    gate_act = jax.nn.silu(z_in[0].astype(jnp.float32)).reshape(tokens, local_heads, P_SIZE)
    gated = (
        (mixed * gate_act * live_mask[:, None, None])
        .reshape(1, tokens, local_heads * P_SIZE)
        .astype(jnp.bfloat16)
    )
    return (gated, end_state[None, None])


def solution(mesh):
    return build(mesh)


def build(mesh):
    return jax.shard_map(
        device_body,
        mesh=mesh,
        in_specs=(
            P("req", "ctx", "head"),
            P("req", "ctx", None),
            P("req", "ctx", "head"),
            P("req", "head", "ctx"),
            P("head"),
            P("head"),
            P("head"),
            P(None, "head"),
            P(),
            P(("ctx", "req"), "head", None, None),
            P(("ctx", "req"), None, "head"),
            P("req", None, None),
            P(None, "head"),
            P(),
        ),
        out_specs=(P("req", "ctx", "head"), P("req", "ctx", "head", None, None)),
        check_vma=False,
    )
```

```python
from functools import partial

import jax
import jax.numpy as jnp
from jax import lax
from jax.sharding import PartitionSpec as P

H = 256
P_SIZE = 64
N = 256
G = 8
K = 4
STRETCH = 256
CHUNKS = 4


HIGHEST = lax.Precision.HIGHEST


def passed_along(value, axis, steps):
    count = lax.axis_size(axis)
    initial, last = (max(0, -steps), min(count, count - steps))
    return lax.ppermute(value, axis, [(source, source + steps) for source in range(initial, last)])


def causal_conv(prev_rows, rows, taps):
    padded = jnp.concatenate([prev_rows, rows.astype(jnp.float32)], axis=0)
    count = rows.shape[0]
    total = taps[0] * padded[0:count]
    for offset in range(1, taps.shape[0]):
        total = total + taps[offset] * padded[offset : offset + count]
    return jax.nn.silu(total).astype(jnp.bfloat16)


def block_state(running, x_blk, b_blk, step_blk, cum):
    block_len, head_count = x_blk.shape[0], x_blk.shape[1]
    group_count = b_blk.shape[1]
    per_group = head_count // group_count
    block_end = cum[:, -1:]
    factor = step_blk * jnp.exp(-(block_end - cum))
    weighted = (x_blk.astype(jnp.float32) * factor.T[:, :, None]).astype(jnp.bfloat16)
    weighted_view = weighted.reshape(block_len, group_count, per_group, running.shape[1])
    contrib = jnp.einsum(
        "qgjp,qgn->gjpn", weighted_view, b_blk, preferred_element_type=jnp.float32
    ).reshape(running.shape)
    return jnp.exp(-cum[:, -1])[:, None, None] * running + contrib


def block_intra(x_blk, b_blk, c_blk, step_blk, cum, skip_gain):
    block_len = x_blk.shape[0]
    head_count = x_blk.shape[1]
    scores = jnp.einsum("qgn,sgn->gqs", c_blk, b_blk, preferred_element_type=jnp.float32)
    group_count = scores.shape[0]
    per_group = head_count // group_count
    scores_h = jnp.broadcast_to(
        scores[:, None], (group_count, per_group, block_len, block_len)
    ).reshape(head_count, block_len, block_len)
    row_ids = lax.broadcasted_iota(jnp.int32, (block_len, block_len), 0)
    col_ids = lax.broadcasted_iota(jnp.int32, (block_len, block_len), 1)
    causal = (row_ids >= col_ids)[None]
    decay_gap = jnp.where(causal, cum[:, :, None] - cum[:, None, :], 0.0)
    decay_mask = jnp.where(causal, jnp.exp(-decay_gap), 0.0)
    weights = (scores_h * decay_mask * step_blk[:, None, :]).astype(jnp.bfloat16)
    y_intra = jnp.einsum("hqs,shp->qhp", weights, x_blk, preferred_element_type=jnp.float32)
    return y_intra, skip_gain[None, :, None] * x_blk.astype(jnp.float32)


def block_from_state(running, c_blk, cum):
    block_len = c_blk.shape[0]
    group_count = c_blk.shape[1]
    head_count = running.shape[0]
    per_group = head_count // group_count
    state_view = running.reshape(group_count, per_group, running.shape[1], running.shape[2])
    y_state = jnp.einsum("qgn,gjpn->qgjp", c_blk.astype(jnp.float32), state_view, precision=HIGHEST)
    return y_state.reshape(block_len, head_count, running.shape[1]) * jnp.exp(-cum).T[:, :, None]


def on_device(
    x_in,
    bc_in,
    z_in,
    dt_raw,
    dt_bias,
    decay_rate,
    skip_gain,
    conv_x,
    conv_bc,
    ssm_pool,
    conv_pool,
    bc_cache,
    owner,
    lengths,
):
    n_ctx = lax.axis_size("ctx")
    n_req = lax.axis_size("req")
    ctx_pos = lax.axis_index("ctx")
    head_pos = lax.axis_index("head")
    req_pos = lax.axis_index("req")
    local_heads = dt_raw.shape[1]
    tokens = x_in.shape[1]
    at_start = ctx_pos == 0

    want = owner[req_pos, 0]
    on_chip = (want // n_req) == ctx_pos
    mine = (want % n_req) == req_pos
    swap = [(src, n_req - 1 - src) for src in range(n_req)]
    other_pool, other_conv = lax.ppermute((ssm_pool[0], conv_pool[0]), "req", swap)
    state_pick = jnp.where(on_chip, jnp.where(mine, ssm_pool[0], other_pool), 0.0)
    conv_pick = jnp.where(on_chip, jnp.where(mine, conv_pool[0], other_conv), 0.0)
    state_pick, x_in, bc_in, z_in, dt_raw = lax.optimization_barrier(
        (state_pick, x_in, bc_in, z_in, dt_raw)
    )
    first_state = lax.psum(state_pick, "ctx")

    positions = ctx_pos * tokens + lax.iota(jnp.int32, tokens)
    live_mask = (positions < lengths[req_pos]).astype(jnp.float32)
    step_size = jax.nn.softplus(dt_raw[0] + dt_bias[:, None]) * live_mask[None, :]
    log_decay = step_size * decay_rate[:, None]
    own_decay = jnp.exp(-jnp.sum(log_decay, axis=1))
    width = conv_pick.shape[1]
    decay_row = jnp.zeros((1, width), jnp.float32).at[0, :local_heads].set(own_decay)
    message = jnp.concatenate([conv_pick, decay_row], axis=0)
    first_conv = conv_pick
    decay_before = jnp.ones_like(own_decay)
    for shift in range(1, n_ctx):
        got_msg = lax.ppermute(
            message, "ctx", [(src, (src + shift) % n_ctx) for src in range(n_ctx)]
        )
        first_conv = first_conv + got_msg[: K - 1]
        decay_before = decay_before * jnp.where(
            shift <= ctx_pos, got_msg[K - 1, :local_heads], 1.0
        )

    tail_x = x_in[0, tokens - (K - 1) :, :]
    tail_bc = bc_in[0, tokens - (K - 1) :, :]
    prev_x, prev_bc = passed_along((tail_x, tail_bc), "ctx", 1)
    prev_x = jnp.where(at_start, first_conv, prev_x.astype(jnp.float32))
    prev_bc = jnp.where(at_start, bc_cache[0], prev_bc.astype(jnp.float32))
    per_group = H // G
    local_groups = max(1, local_heads // per_group)
    group_start = head_pos * local_heads // per_group
    span = local_groups * N

    def pick_groups(values):
        input_cols = lax.dynamic_slice_in_dim(values, group_start * N, span, 1)
        output_cols = lax.dynamic_slice_in_dim(values, G * N + group_start * N, span, 1)
        return jnp.concatenate([input_cols, output_cols], axis=1)

    x_head = causal_conv(prev_x, x_in[0, : K - 1], conv_x)
    x_rest = causal_conv(x_in[0, : K - 1].astype(jnp.float32), x_in[0, K - 1 :], conv_x)
    x_conv = jnp.concatenate([x_head, x_rest], axis=0)
    bc_conv = causal_conv(pick_groups(prev_bc), pick_groups(bc_in[0]), pick_groups(conv_bc))
    blocks = tokens // STRETCH
    x_view = x_conv.reshape(blocks, STRETCH, local_heads, P_SIZE)
    b_view = bc_conv[:, :span].reshape(blocks, STRETCH, local_groups, N)
    c_view = bc_conv[:, span:].reshape(blocks, STRETCH, local_groups, N)
    step_view = step_size.reshape(local_heads, blocks, STRETCH).transpose(1, 0, 2)
    log_view = log_decay.reshape(local_heads, blocks, STRETCH).transpose(1, 0, 2)
    cum_view = jnp.cumsum(log_view, axis=2)

    running = jnp.zeros((local_heads, P_SIZE, N), jnp.float32)
    starts = []
    for blk in range(blocks):
        starts.append(running)
        running = block_state(running, x_view[blk], b_view[blk], step_view[blk], cum_view[blk])
    local_end = running

    intra = [
        block_intra(x_view[blk], b_view[blk], c_view[blk], step_view[blk], cum_view[blk], skip_gain)
        for blk in range(blocks)
    ]

    local_end, later_intra = lax.optimization_barrier((local_end, intra[1:]))
    intra = intra[:1] + list(later_intra)

    chunk = local_heads // CHUNKS
    end_chunks = local_end.reshape(CHUNKS, chunk, P_SIZE, N)
    decay_chunks = own_decay.reshape(CHUNKS, chunk)
    got = jnp.zeros((chunk, P_SIZE, N), jnp.float32)
    received = []
    for step in range(n_ctx + CHUNKS - 2):
        index = jnp.clip(step - ctx_pos, 0, CHUNKS - 1)
        sent = (
            lax.dynamic_index_in_dim(decay_chunks, index, keepdims=False)[:, None, None] * got
            + lax.dynamic_index_in_dim(end_chunks, index, keepdims=False)
        )
        pairs = [
            (src, src + 1)
            for src in range(max(0, step - CHUNKS + 1), min(step, n_ctx - 2) + 1)
        ]
        got = lax.ppermute(sent.astype(jnp.bfloat16), "ctx", pairs).astype(jnp.float32)
        received.append(got)
    received = jnp.stack(received)
    prefix = lax.dynamic_slice_in_dim(received, jnp.maximum(ctx_pos - 1, 0), CHUNKS, 0)
    prefix = jnp.where(at_start, 0.0, prefix.reshape(local_heads, P_SIZE, N))
    start_state = prefix + decay_before[:, None, None] * first_state
    end_state = own_decay[:, None, None] * start_state + local_end

    outs = []
    for blk in range(blocks):
        y_intra, y_skip = intra[blk]
        outs.append(y_intra + block_from_state(starts[blk], c_view[blk], cum_view[blk]) + y_skip)
    local_out = jnp.concatenate(outs, axis=0)

    cum_dev = jnp.cumsum(log_decay, axis=1)
    readout = bc_conv[:, span:].reshape(tokens, local_groups, N)
    start_view = start_state.reshape(local_groups, local_heads // local_groups, P_SIZE, N)
    carried = jnp.einsum(
        "tgn,gjpn->tgjp", readout.astype(jnp.float32), start_view, precision=HIGHEST
    )
    carried = carried.reshape(tokens, local_heads, P_SIZE) * jnp.exp(-cum_dev).T[:, :, None]
    mixed = local_out + carried
    gate_act = jax.nn.silu(z_in[0].astype(jnp.float32)).reshape(tokens, local_heads, P_SIZE)
    gated = (
        (mixed * gate_act * live_mask[:, None, None])
        .reshape(1, tokens, local_heads * P_SIZE)
        .astype(jnp.bfloat16)
    )
    return (gated, end_state[None, None])


def solution(mesh):
    return jax.shard_map(
        on_device,
        mesh=mesh,
        in_specs=(
            P("req", "ctx", "head"),
            P("req", "ctx", None),
            P("req", "ctx", "head"),
            P("req", "head", "ctx"),
            P("head"),
            P("head"),
            P("head"),
            P(None, "head"),
            P(),
            P(("ctx", "req"), "head", None, None),
            P(("ctx", "req"), None, "head"),
            P("req", None, None),
            P(None, "head"),
            P(),
        ),
        out_specs=(P("req", "ctx", "head"), P("req", "ctx", "head", None, None)),
        check_vma=False,
    )
```

```python
from functools import partial

import jax
import jax.numpy as jnp
from jax import lax
from jax.sharding import PartitionSpec as P

H = 256
P_SIZE = 64
N = 256
G = 8
K = 4
STRETCH = 256
CHUNKS = 4


HIGHEST = lax.Precision.HIGHEST


def passed_along(value, axis, steps):
    count = lax.axis_size(axis)
    initial, last = (max(0, -steps), min(count, count - steps))
    return lax.ppermute(value, axis, [(source, source + steps) for source in range(initial, last)])


def causal_conv(prev_rows, rows, taps):
    padded = jnp.concatenate([prev_rows, rows.astype(jnp.float32)], axis=0)
    count = rows.shape[0]
    total = taps[0] * padded[0:count]
    for offset in range(1, taps.shape[0]):
        total = total + taps[offset] * padded[offset : offset + count]
    return jax.nn.silu(total).astype(jnp.bfloat16)


def block_state(running, x_blk, b_blk, step_blk, cum):
    block_len, head_count = x_blk.shape[0], x_blk.shape[1]
    group_count = b_blk.shape[1]
    per_group = head_count // group_count
    block_end = cum[:, -1:]
    factor = step_blk * jnp.exp(-(block_end - cum))
    weighted = (x_blk.astype(jnp.float32) * factor.T[:, :, None]).astype(jnp.bfloat16)
    weighted_view = weighted.reshape(block_len, group_count, per_group, running.shape[1])
    contrib = jnp.einsum(
        "qgjp,qgn->gjpn", weighted_view, b_blk, preferred_element_type=jnp.float32
    ).reshape(running.shape)
    return jnp.exp(-cum[:, -1])[:, None, None] * running + contrib


def block_intra(x_blk, b_blk, c_blk, step_blk, cum, skip_gain):
    block_len = x_blk.shape[0]
    head_count = x_blk.shape[1]
    scores = jnp.einsum("qgn,sgn->gqs", c_blk, b_blk, preferred_element_type=jnp.float32)
    group_count = scores.shape[0]
    per_group = head_count // group_count
    scores_h = jnp.broadcast_to(
        scores[:, None], (group_count, per_group, block_len, block_len)
    ).reshape(head_count, block_len, block_len)
    row_ids = lax.broadcasted_iota(jnp.int32, (block_len, block_len), 0)
    col_ids = lax.broadcasted_iota(jnp.int32, (block_len, block_len), 1)
    causal = (row_ids >= col_ids)[None]
    decay_gap = jnp.where(causal, cum[:, :, None] - cum[:, None, :], 0.0)
    decay_mask = jnp.where(causal, jnp.exp(-decay_gap), 0.0)
    weights = (scores_h * decay_mask * step_blk[:, None, :]).astype(jnp.bfloat16)
    y_intra = jnp.einsum("hqs,shp->qhp", weights, x_blk, preferred_element_type=jnp.float32)
    return y_intra, skip_gain[None, :, None] * x_blk.astype(jnp.float32)


def block_from_state(running, c_blk, cum):
    block_len = c_blk.shape[0]
    group_count = c_blk.shape[1]
    head_count = running.shape[0]
    per_group = head_count // group_count
    state_view = running.reshape(group_count, per_group, running.shape[1], running.shape[2])
    y_state = jnp.einsum("qgn,gjpn->qgjp", c_blk.astype(jnp.float32), state_view, precision=HIGHEST)
    return y_state.reshape(block_len, head_count, running.shape[1]) * jnp.exp(-cum).T[:, :, None]


def on_device(
    x_in,
    bc_in,
    z_in,
    dt_raw,
    dt_bias,
    decay_rate,
    skip_gain,
    conv_x,
    conv_bc,
    ssm_pool,
    conv_pool,
    bc_cache,
    owner,
    lengths,
):
    n_ctx = lax.axis_size("ctx")
    n_req = lax.axis_size("req")
    ctx_pos = lax.axis_index("ctx")
    head_pos = lax.axis_index("head")
    req_pos = lax.axis_index("req")
    local_heads = dt_raw.shape[1]
    tokens = x_in.shape[1]
    at_start = ctx_pos == 0

    want = owner[req_pos, 0]
    on_chip = (want // n_req) == ctx_pos
    mine = (want % n_req) == req_pos
    swap = [(src, n_req - 1 - src) for src in range(n_req)]
    other_pool, other_conv = lax.ppermute((ssm_pool[0], conv_pool[0]), "req", swap)
    state_pick = jnp.where(on_chip, jnp.where(mine, ssm_pool[0], other_pool), 0.0)
    conv_pick = jnp.where(on_chip, jnp.where(mine, conv_pool[0], other_conv), 0.0)
    state_pick, x_in, bc_in, z_in, dt_raw = lax.optimization_barrier(
        (state_pick, x_in, bc_in, z_in, dt_raw)
    )
    first_state = lax.psum(state_pick, "ctx")

    positions = ctx_pos * tokens + lax.iota(jnp.int32, tokens)
    live_mask = (positions < lengths[req_pos]).astype(jnp.float32)
    step_size = jax.nn.softplus(dt_raw[0] + dt_bias[:, None]) * live_mask[None, :]
    log_decay = step_size * decay_rate[:, None]
    own_decay = jnp.exp(-jnp.sum(log_decay, axis=1))
    width = conv_pick.shape[1]
    decay_row = jnp.zeros((1, width), jnp.float32).at[0, :local_heads].set(own_decay)
    message = jnp.concatenate([conv_pick, decay_row], axis=0)
    gathered = message[None]
    shift = 1
    while shift < n_ctx:
        got_msg = lax.ppermute(
            gathered, "ctx", [(src, (src + shift) % n_ctx) for src in range(n_ctx)]
        )
        gathered = jnp.concatenate([gathered, got_msg], axis=0)
        shift *= 2
    first_conv = jnp.sum(gathered[:, : K - 1], axis=0)
    earlier = (lax.iota(jnp.int32, n_ctx) <= ctx_pos) & (lax.iota(jnp.int32, n_ctx) > 0)
    decay_before = jnp.prod(
        jnp.where(earlier[:, None], gathered[:, K - 1, :local_heads], 1.0), axis=0
    )

    tail_x = x_in[0, tokens - (K - 1) :, :]
    tail_bc = bc_in[0, tokens - (K - 1) :, :]
    prev_x, prev_bc = passed_along((tail_x, tail_bc), "ctx", 1)
    prev_x = jnp.where(at_start, first_conv, prev_x.astype(jnp.float32))
    prev_bc = jnp.where(at_start, bc_cache[0], prev_bc.astype(jnp.float32))
    per_group = H // G
    local_groups = max(1, local_heads // per_group)
    group_start = head_pos * local_heads // per_group
    span = local_groups * N

    def pick_groups(values):
        input_cols = lax.dynamic_slice_in_dim(values, group_start * N, span, 1)
        output_cols = lax.dynamic_slice_in_dim(values, G * N + group_start * N, span, 1)
        return jnp.concatenate([input_cols, output_cols], axis=1)

    x_head = causal_conv(prev_x, x_in[0, : K - 1], conv_x)
    x_rest = causal_conv(x_in[0, : K - 1].astype(jnp.float32), x_in[0, K - 1 :], conv_x)
    x_conv = jnp.concatenate([x_head, x_rest], axis=0)
    bc_conv = causal_conv(pick_groups(prev_bc), pick_groups(bc_in[0]), pick_groups(conv_bc))
    blocks = tokens // STRETCH
    x_view = x_conv.reshape(blocks, STRETCH, local_heads, P_SIZE)
    b_view = bc_conv[:, :span].reshape(blocks, STRETCH, local_groups, N)
    c_view = bc_conv[:, span:].reshape(blocks, STRETCH, local_groups, N)
    step_view = step_size.reshape(local_heads, blocks, STRETCH).transpose(1, 0, 2)
    log_view = log_decay.reshape(local_heads, blocks, STRETCH).transpose(1, 0, 2)
    cum_view = jnp.cumsum(log_view, axis=2)

    running = jnp.zeros((local_heads, P_SIZE, N), jnp.float32)
    starts = []
    for blk in range(blocks):
        starts.append(running)
        running = block_state(running, x_view[blk], b_view[blk], step_view[blk], cum_view[blk])
    local_end = running

    intra = [
        block_intra(x_view[blk], b_view[blk], c_view[blk], step_view[blk], cum_view[blk], skip_gain)
        for blk in range(blocks)
    ]

    local_end, later_intra = lax.optimization_barrier((local_end, intra[1:]))
    intra = intra[:1] + list(later_intra)

    chunk = local_heads // CHUNKS
    end_chunks = local_end.reshape(CHUNKS, chunk, P_SIZE, N)
    decay_chunks = own_decay.reshape(CHUNKS, chunk)
    got = jnp.zeros((chunk, P_SIZE, N), jnp.float32)
    received = []
    for step in range(n_ctx + CHUNKS - 2):
        index = jnp.clip(step - ctx_pos, 0, CHUNKS - 1)
        sent = (
            lax.dynamic_index_in_dim(decay_chunks, index, keepdims=False)[:, None, None] * got
            + lax.dynamic_index_in_dim(end_chunks, index, keepdims=False)
        )
        pairs = [
            (src, src + 1)
            for src in range(max(0, step - CHUNKS + 1), min(step, n_ctx - 2) + 1)
        ]
        got = lax.ppermute(sent.astype(jnp.bfloat16), "ctx", pairs).astype(jnp.float32)
        received.append(got)
    received = jnp.stack(received)
    prefix = lax.dynamic_slice_in_dim(received, jnp.maximum(ctx_pos - 1, 0), CHUNKS, 0)
    prefix = jnp.where(at_start, 0.0, prefix.reshape(local_heads, P_SIZE, N))
    start_state = prefix + decay_before[:, None, None] * first_state
    end_state = own_decay[:, None, None] * start_state + local_end

    outs = []
    for blk in range(blocks):
        y_intra, y_skip = intra[blk]
        outs.append(y_intra + block_from_state(starts[blk], c_view[blk], cum_view[blk]) + y_skip)
    local_out = jnp.concatenate(outs, axis=0)

    cum_dev = jnp.cumsum(log_decay, axis=1)
    readout = bc_conv[:, span:].reshape(tokens, local_groups, N)
    start_view = start_state.reshape(local_groups, local_heads // local_groups, P_SIZE, N)
    carried = jnp.einsum(
        "tgn,gjpn->tgjp", readout.astype(jnp.float32), start_view, precision=HIGHEST
    )
    carried = carried.reshape(tokens, local_heads, P_SIZE) * jnp.exp(-cum_dev).T[:, :, None]
    mixed = local_out + carried
    gate_act = jax.nn.silu(z_in[0].astype(jnp.float32)).reshape(tokens, local_heads, P_SIZE)
    gated = (
        (mixed * gate_act * live_mask[:, None, None])
        .reshape(1, tokens, local_heads * P_SIZE)
        .astype(jnp.bfloat16)
    )
    return (gated, end_state[None, None])


def solution(mesh):
    return jax.shard_map(
        on_device,
        mesh=mesh,
        in_specs=(
            P("req", "ctx", "head"),
            P("req", "ctx", None),
            P("req", "ctx", "head"),
            P("req", "head", "ctx"),
            P("head"),
            P("head"),
            P("head"),
            P(None, "head"),
            P(),
            P(("ctx", "req"), "head", None, None),
            P(("ctx", "req"), None, "head"),
            P("req", None, None),
            P(None, "head"),
            P(),
        ),
        out_specs=(P("req", "ctx", "head"), P("req", "ctx", "head", None, None)),
        check_vma=False,
    )
```

```python
from functools import partial

import jax
import jax.numpy as jnp
from jax import lax
from jax.sharding import PartitionSpec as P

H = 256
P_SIZE = 64
N = 256
G = 8
K = 4
STRETCH = 256
CHUNKS = 4


HIGHEST = lax.Precision.HIGHEST


def passed_along(value, axis, steps):
    count = lax.axis_size(axis)
    initial, last = (max(0, -steps), min(count, count - steps))
    return lax.ppermute(value, axis, [(source, source + steps) for source in range(initial, last)])


def causal_conv(prev_rows, rows, taps):
    padded = jnp.concatenate([prev_rows, rows.astype(jnp.float32)], axis=0)
    count = rows.shape[0]
    total = taps[0] * padded[0:count]
    for offset in range(1, taps.shape[0]):
        total = total + taps[offset] * padded[offset : offset + count]
    return jax.nn.silu(total).astype(jnp.bfloat16)


def block_state(running, x_blk, b_blk, step_blk, cum):
    block_len, head_count = x_blk.shape[0], x_blk.shape[1]
    group_count = b_blk.shape[1]
    per_group = head_count // group_count
    block_end = cum[:, -1:]
    factor = step_blk * jnp.exp(-(block_end - cum))
    weighted = (x_blk.astype(jnp.float32) * factor.T[:, :, None]).astype(jnp.bfloat16)
    weighted_view = weighted.reshape(block_len, group_count, per_group, running.shape[1])
    contrib = jnp.einsum(
        "qgjp,qgn->gjpn", weighted_view, b_blk, preferred_element_type=jnp.float32
    ).reshape(running.shape)
    return jnp.exp(-cum[:, -1])[:, None, None] * running + contrib


def block_intra(x_blk, b_blk, c_blk, step_blk, cum, skip_gain):
    block_len = x_blk.shape[0]
    head_count = x_blk.shape[1]
    scores = jnp.einsum("qgn,sgn->gqs", c_blk, b_blk, preferred_element_type=jnp.float32)
    group_count = scores.shape[0]
    per_group = head_count // group_count
    scores_h = jnp.broadcast_to(
        scores[:, None], (group_count, per_group, block_len, block_len)
    ).reshape(head_count, block_len, block_len)
    row_ids = lax.broadcasted_iota(jnp.int32, (block_len, block_len), 0)
    col_ids = lax.broadcasted_iota(jnp.int32, (block_len, block_len), 1)
    causal = (row_ids >= col_ids)[None]
    decay_gap = jnp.where(causal, cum[:, :, None] - cum[:, None, :], 0.0)
    decay_mask = jnp.where(causal, jnp.exp(-decay_gap), 0.0)
    weights = (scores_h * decay_mask * step_blk[:, None, :]).astype(jnp.bfloat16)
    y_intra = jnp.einsum("hqs,shp->qhp", weights, x_blk, preferred_element_type=jnp.float32)
    return y_intra, skip_gain[None, :, None] * x_blk.astype(jnp.float32)


def block_from_state(running, c_blk, cum):
    block_len = c_blk.shape[0]
    group_count = c_blk.shape[1]
    head_count = running.shape[0]
    per_group = head_count // group_count
    state_view = running.reshape(group_count, per_group, running.shape[1], running.shape[2])
    y_state = jnp.einsum("qgn,gjpn->qgjp", c_blk.astype(jnp.float32), state_view, precision=HIGHEST)
    return y_state.reshape(block_len, head_count, running.shape[1]) * jnp.exp(-cum).T[:, :, None]


def on_device(
    x_in,
    bc_in,
    z_in,
    dt_raw,
    dt_bias,
    decay_rate,
    skip_gain,
    conv_x,
    conv_bc,
    ssm_pool,
    conv_pool,
    bc_cache,
    owner,
    lengths,
):
    n_ctx = lax.axis_size("ctx")
    n_req = lax.axis_size("req")
    ctx_pos = lax.axis_index("ctx")
    head_pos = lax.axis_index("head")
    req_pos = lax.axis_index("req")
    local_heads = dt_raw.shape[1]
    tokens = x_in.shape[1]
    at_start = ctx_pos == 0

    want = owner[req_pos, 0]
    on_chip = (want // n_req) == ctx_pos
    mine = (want % n_req) == req_pos
    swap = [(src, n_req - 1 - src) for src in range(n_req)]
    other_pool, other_conv = lax.ppermute((ssm_pool[0], conv_pool[0]), "req", swap)
    state_pick = jnp.where(on_chip, jnp.where(mine, ssm_pool[0], other_pool), 0.0)
    conv_pick = jnp.where(on_chip, jnp.where(mine, conv_pool[0], other_conv), 0.0)
    state_pick, x_in, bc_in, z_in, dt_raw = lax.optimization_barrier(
        (state_pick, x_in, bc_in, z_in, dt_raw)
    )
    first_state = lax.psum(state_pick, "ctx")

    positions = ctx_pos * tokens + lax.iota(jnp.int32, tokens)
    live_mask = (positions < lengths[req_pos]).astype(jnp.float32)
    step_size = jax.nn.softplus(dt_raw[0] + dt_bias[:, None]) * live_mask[None, :]
    log_decay = step_size * decay_rate[:, None]
    own_decay = jnp.exp(-jnp.sum(log_decay, axis=1))
    width = conv_pick.shape[1]
    decay_row = jnp.zeros((1, width), jnp.float32).at[0, :local_heads].set(own_decay)
    message = jnp.concatenate([conv_pick, decay_row], axis=0)
    first_conv = conv_pick
    decay_before = jnp.ones_like(own_decay)
    for shift in range(1, n_ctx):
        got_msg = lax.ppermute(
            message, "ctx", [(src, (src + shift) % n_ctx) for src in range(n_ctx)]
        )
        first_conv = first_conv + got_msg[: K - 1]
        decay_before = decay_before * jnp.where(
            shift <= ctx_pos, got_msg[K - 1, :local_heads], 1.0
        )

    tail_x = x_in[0, tokens - (K - 1) :, :]
    tail_bc = bc_in[0, tokens - (K - 1) :, :]
    prev_x, prev_bc = passed_along((tail_x, tail_bc), "ctx", 1)
    prev_x = jnp.where(at_start, first_conv, prev_x.astype(jnp.float32))
    prev_bc = jnp.where(at_start, bc_cache[0], prev_bc.astype(jnp.float32))
    per_group = H // G
    local_groups = max(1, local_heads // per_group)
    group_start = head_pos * local_heads // per_group
    span = local_groups * N

    def pick_groups(values):
        input_cols = lax.dynamic_slice_in_dim(values, group_start * N, span, 1)
        output_cols = lax.dynamic_slice_in_dim(values, G * N + group_start * N, span, 1)
        return jnp.concatenate([input_cols, output_cols], axis=1)

    x_head = causal_conv(prev_x, x_in[0, : K - 1], conv_x)
    x_rest = causal_conv(x_in[0, : K - 1].astype(jnp.float32), x_in[0, K - 1 :], conv_x)
    x_conv = jnp.concatenate([x_head, x_rest], axis=0)
    bc_conv = causal_conv(pick_groups(prev_bc), pick_groups(bc_in[0]), pick_groups(conv_bc))
    blocks = tokens // STRETCH
    x_view = x_conv.reshape(blocks, STRETCH, local_heads, P_SIZE)
    b_view = bc_conv[:, :span].reshape(blocks, STRETCH, local_groups, N)
    c_view = bc_conv[:, span:].reshape(blocks, STRETCH, local_groups, N)
    step_view = step_size.reshape(local_heads, blocks, STRETCH).transpose(1, 0, 2)
    log_view = log_decay.reshape(local_heads, blocks, STRETCH).transpose(1, 0, 2)
    cum_view = jnp.cumsum(log_view, axis=2)

    running = jnp.zeros((local_heads, P_SIZE, N), jnp.float32)
    starts = []
    for blk in range(blocks):
        starts.append(running)
        running = block_state(running, x_view[blk], b_view[blk], step_view[blk], cum_view[blk])
    local_end = running

    intra = [
        block_intra(x_view[blk], b_view[blk], c_view[blk], step_view[blk], cum_view[blk], skip_gain)
        for blk in range(blocks)
    ]

    local_end, later_intra = lax.optimization_barrier((local_end, intra[1:]))
    intra = intra[:1] + list(later_intra)

    chunk = local_heads // CHUNKS
    end_chunks = local_end.reshape(CHUNKS, chunk, P_SIZE, N)
    decay_chunks = own_decay.reshape(CHUNKS, chunk)
    got = jnp.zeros((chunk, P_SIZE, N), jnp.float32)
    received = []
    for step in range(n_ctx + CHUNKS - 2):
        index = jnp.clip(step - ctx_pos, 0, CHUNKS - 1)
        sent = (
            lax.dynamic_index_in_dim(decay_chunks, index, keepdims=False)[:, None, None] * got
            + lax.dynamic_index_in_dim(end_chunks, index, keepdims=False)
        )
        pairs = [
            (src, src + 1)
            for src in range(max(0, step - CHUNKS + 1), min(step, n_ctx - 2) + 1)
        ]
        got = lax.ppermute(sent.astype(jnp.bfloat16), "ctx", pairs).astype(jnp.float32)
        received.append(got)
    received = jnp.stack(received)
    prefix = lax.dynamic_slice_in_dim(received, jnp.maximum(ctx_pos - 1, 0), CHUNKS, 0)
    prefix = jnp.where(at_start, 0.0, prefix.reshape(local_heads, P_SIZE, N))
    start_state = prefix + decay_before[:, None, None] * first_state
    end_state = own_decay[:, None, None] * start_state + local_end

    outs = []
    for blk in range(blocks):
        y_intra, y_skip = intra[blk]
        outs.append(y_intra + block_from_state(starts[blk], c_view[blk], cum_view[blk]) + y_skip)
    local_out = jnp.concatenate(outs, axis=0)

    block_totals = cum_view[:, :, -1]
    offsets = jnp.concatenate(
        [jnp.zeros_like(block_totals[:1]), jnp.cumsum(block_totals[:-1], axis=0)], axis=0
    )
    cum_dev = (cum_view + offsets[:, :, None]).transpose(1, 0, 2).reshape(local_heads, tokens)
    readout = bc_conv[:, span:].reshape(tokens, local_groups, N)
    start_view = start_state.reshape(local_groups, local_heads // local_groups, P_SIZE, N)
    carried = jnp.einsum(
        "tgn,gjpn->tgjp", readout.astype(jnp.float32), start_view, precision=HIGHEST
    )
    carried = carried.reshape(tokens, local_heads, P_SIZE) * jnp.exp(-cum_dev).T[:, :, None]
    mixed = local_out + carried
    gate_act = jax.nn.silu(z_in[0].astype(jnp.float32)).reshape(tokens, local_heads, P_SIZE)
    gated = (
        (mixed * gate_act * live_mask[:, None, None])
        .reshape(1, tokens, local_heads * P_SIZE)
        .astype(jnp.bfloat16)
    )
    return (gated, end_state[None, None])


def solution(mesh):
    return jax.shard_map(
        on_device,
        mesh=mesh,
        in_specs=(
            P("req", "ctx", "head"),
            P("req", "ctx", None),
            P("req", "ctx", "head"),
            P("req", "head", "ctx"),
            P("head"),
            P("head"),
            P("head"),
            P(None, "head"),
            P(),
            P(("ctx", "req"), "head", None, None),
            P(("ctx", "req"), None, "head"),
            P("req", None, None),
            P(None, "head"),
            P(),
        ),
        out_specs=(P("req", "ctx", "head"), P("req", "ctx", "head", None, None)),
        check_vma=False,
    )
```

```python
from functools import partial

import jax
import jax.numpy as jnp
from jax import lax
from jax.sharding import PartitionSpec as P

H = 256
P_SIZE = 64
N = 256
G = 8
K = 4
STRETCH = 256
CHUNKS = 4


HIGHEST = lax.Precision.HIGHEST


def passed_along(value, axis, steps):
    count = lax.axis_size(axis)
    initial, last = (max(0, -steps), min(count, count - steps))
    return lax.ppermute(value, axis, [(source, source + steps) for source in range(initial, last)])


def causal_conv(prev_rows, rows, taps):
    padded = jnp.concatenate([prev_rows, rows.astype(jnp.float32)], axis=0)
    count = rows.shape[0]
    total = taps[0] * padded[0:count]
    for offset in range(1, taps.shape[0]):
        total = total + taps[offset] * padded[offset : offset + count]
    return jax.nn.silu(total).astype(jnp.bfloat16)


def block_state(running, x_blk, b_blk, step_blk, cum):
    block_len, head_count = x_blk.shape[0], x_blk.shape[1]
    group_count = b_blk.shape[1]
    per_group = head_count // group_count
    block_end = cum[:, -1:]
    factor = step_blk * jnp.exp(-(block_end - cum))
    weighted = (x_blk.astype(jnp.float32) * factor.T[:, :, None]).astype(jnp.bfloat16)
    weighted_view = weighted.reshape(block_len, group_count, per_group, running.shape[1])
    contrib = jnp.einsum(
        "qgjp,qgn->gjpn", weighted_view, b_blk, preferred_element_type=jnp.float32
    ).reshape(running.shape)
    return jnp.exp(-cum[:, -1])[:, None, None] * running + contrib


def block_intra(x_blk, b_blk, c_blk, step_blk, cum, skip_gain):
    block_len = x_blk.shape[0]
    head_count = x_blk.shape[1]
    scores = jnp.einsum("qgn,sgn->gqs", c_blk, b_blk, preferred_element_type=jnp.float32)
    group_count = scores.shape[0]
    per_group = head_count // group_count
    scores_h = jnp.broadcast_to(
        scores[:, None], (group_count, per_group, block_len, block_len)
    ).reshape(head_count, block_len, block_len)
    row_ids = lax.broadcasted_iota(jnp.int32, (block_len, block_len), 0)
    col_ids = lax.broadcasted_iota(jnp.int32, (block_len, block_len), 1)
    causal = (row_ids >= col_ids)[None]
    decay_gap = jnp.where(causal, cum[:, :, None] - cum[:, None, :], 0.0)
    decay_mask = jnp.where(causal, jnp.exp(-decay_gap), 0.0)
    weights = (scores_h * decay_mask * step_blk[:, None, :]).astype(jnp.bfloat16)
    y_intra = jnp.einsum("hqs,shp->qhp", weights, x_blk, preferred_element_type=jnp.float32)
    return y_intra, skip_gain[None, :, None] * x_blk.astype(jnp.float32)


def block_from_state(running, c_blk, cum):
    block_len = c_blk.shape[0]
    group_count = c_blk.shape[1]
    head_count = running.shape[0]
    per_group = head_count // group_count
    state_view = running.reshape(group_count, per_group, running.shape[1], running.shape[2])
    y_state = jnp.einsum("qgn,gjpn->qgjp", c_blk.astype(jnp.float32), state_view, precision=HIGHEST)
    return y_state.reshape(block_len, head_count, running.shape[1]) * jnp.exp(-cum).T[:, :, None]


def on_device(
    x_in,
    bc_in,
    z_in,
    dt_raw,
    dt_bias,
    decay_rate,
    skip_gain,
    conv_x,
    conv_bc,
    ssm_pool,
    conv_pool,
    bc_cache,
    owner,
    lengths,
):
    n_ctx = lax.axis_size("ctx")
    n_req = lax.axis_size("req")
    ctx_pos = lax.axis_index("ctx")
    head_pos = lax.axis_index("head")
    req_pos = lax.axis_index("req")
    local_heads = dt_raw.shape[1]
    tokens = x_in.shape[1]
    at_start = ctx_pos == 0

    want = owner[req_pos, 0]
    on_chip = (want // n_req) == ctx_pos
    mine = (want % n_req) == req_pos
    swap = [(src, n_req - 1 - src) for src in range(n_req)]
    other_pool, other_conv = lax.ppermute((ssm_pool[0], conv_pool[0]), "req", swap)
    state_pick = jnp.where(on_chip, jnp.where(mine, ssm_pool[0], other_pool), 0.0)
    conv_pick = jnp.where(on_chip, jnp.where(mine, conv_pool[0], other_conv), 0.0)
    state_pick, bc_in, dt_raw = lax.optimization_barrier((state_pick, bc_in, dt_raw))
    first_state = lax.psum(state_pick, "ctx")

    positions = ctx_pos * tokens + lax.iota(jnp.int32, tokens)
    live_mask = (positions < lengths[req_pos]).astype(jnp.float32)
    step_size = jax.nn.softplus(dt_raw[0] + dt_bias[:, None]) * live_mask[None, :]
    log_decay = step_size * decay_rate[:, None]
    own_decay = jnp.exp(-jnp.sum(log_decay, axis=1))
    width = conv_pick.shape[1]
    decay_row = jnp.zeros((1, width), jnp.float32).at[0, :local_heads].set(own_decay)
    message = jnp.concatenate([conv_pick, decay_row], axis=0)
    first_conv = conv_pick
    decay_before = jnp.ones_like(own_decay)
    for shift in range(1, n_ctx):
        got_msg = lax.ppermute(
            message, "ctx", [(src, (src + shift) % n_ctx) for src in range(n_ctx)]
        )
        first_conv = first_conv + got_msg[: K - 1]
        decay_before = decay_before * jnp.where(
            shift <= ctx_pos, got_msg[K - 1, :local_heads], 1.0
        )

    tail_x = x_in[0, tokens - (K - 1) :, :]
    tail_bc = bc_in[0, tokens - (K - 1) :, :]
    prev_x, prev_bc = passed_along((tail_x, tail_bc), "ctx", 1)
    prev_x = jnp.where(at_start, first_conv, prev_x.astype(jnp.float32))
    prev_bc = jnp.where(at_start, bc_cache[0], prev_bc.astype(jnp.float32))
    per_group = H // G
    local_groups = max(1, local_heads // per_group)
    group_start = head_pos * local_heads // per_group
    span = local_groups * N

    def pick_groups(values):
        input_cols = lax.dynamic_slice_in_dim(values, group_start * N, span, 1)
        output_cols = lax.dynamic_slice_in_dim(values, G * N + group_start * N, span, 1)
        return jnp.concatenate([input_cols, output_cols], axis=1)

    x_head = causal_conv(prev_x, x_in[0, : K - 1], conv_x)
    x_rest = causal_conv(x_in[0, : K - 1].astype(jnp.float32), x_in[0, K - 1 :], conv_x)
    x_conv = jnp.concatenate([x_head, x_rest], axis=0)
    bc_conv = causal_conv(pick_groups(prev_bc), pick_groups(bc_in[0]), pick_groups(conv_bc))
    blocks = tokens // STRETCH
    x_view = x_conv.reshape(blocks, STRETCH, local_heads, P_SIZE)
    b_view = bc_conv[:, :span].reshape(blocks, STRETCH, local_groups, N)
    c_view = bc_conv[:, span:].reshape(blocks, STRETCH, local_groups, N)
    step_view = step_size.reshape(local_heads, blocks, STRETCH).transpose(1, 0, 2)
    log_view = log_decay.reshape(local_heads, blocks, STRETCH).transpose(1, 0, 2)
    cum_view = jnp.cumsum(log_view, axis=2)

    running = jnp.zeros((local_heads, P_SIZE, N), jnp.float32)
    starts = []
    for blk in range(blocks):
        starts.append(running)
        running = block_state(running, x_view[blk], b_view[blk], step_view[blk], cum_view[blk])
    local_end = running

    intra = [
        block_intra(x_view[blk], b_view[blk], c_view[blk], step_view[blk], cum_view[blk], skip_gain)
        for blk in range(blocks)
    ]

    local_end, later_intra = lax.optimization_barrier((local_end, intra[1:]))
    intra = intra[:1] + list(later_intra)

    chunk = local_heads // CHUNKS
    end_chunks = local_end.reshape(CHUNKS, chunk, P_SIZE, N)
    decay_chunks = own_decay.reshape(CHUNKS, chunk)
    got = jnp.zeros((chunk, P_SIZE, N), jnp.float32)
    received = []
    for step in range(n_ctx + CHUNKS - 2):
        index = jnp.clip(step - ctx_pos, 0, CHUNKS - 1)
        sent = (
            lax.dynamic_index_in_dim(decay_chunks, index, keepdims=False)[:, None, None] * got
            + lax.dynamic_index_in_dim(end_chunks, index, keepdims=False)
        )
        pairs = [
            (src, src + 1)
            for src in range(max(0, step - CHUNKS + 1), min(step, n_ctx - 2) + 1)
        ]
        got = lax.ppermute(sent.astype(jnp.bfloat16), "ctx", pairs).astype(jnp.float32)
        received.append(got)
    received = jnp.stack(received)
    prefix = lax.dynamic_slice_in_dim(received, jnp.maximum(ctx_pos - 1, 0), CHUNKS, 0)
    prefix = jnp.where(at_start, 0.0, prefix.reshape(local_heads, P_SIZE, N))
    start_state = prefix + decay_before[:, None, None] * first_state
    end_state = own_decay[:, None, None] * start_state + local_end

    outs = []
    for blk in range(blocks):
        y_intra, y_skip = intra[blk]
        outs.append(y_intra + block_from_state(starts[blk], c_view[blk], cum_view[blk]) + y_skip)
    local_out = jnp.concatenate(outs, axis=0)

    block_totals = cum_view[:, :, -1]
    offsets = jnp.concatenate(
        [jnp.zeros_like(block_totals[:1]), jnp.cumsum(block_totals[:-1], axis=0)], axis=0
    )
    cum_dev = (cum_view + offsets[:, :, None]).transpose(1, 0, 2).reshape(local_heads, tokens)
    readout = bc_conv[:, span:].reshape(tokens, local_groups, N)
    start_view = start_state.reshape(local_groups, local_heads // local_groups, P_SIZE, N)
    carried = jnp.einsum(
        "tgn,gjpn->tgjp", readout.astype(jnp.float32), start_view, precision=HIGHEST
    )
    carried = carried.reshape(tokens, local_heads, P_SIZE) * jnp.exp(-cum_dev).T[:, :, None]
    mixed = local_out + carried
    gate_act = jax.nn.silu(z_in[0].astype(jnp.float32)).reshape(tokens, local_heads, P_SIZE)
    gated = (
        (mixed * gate_act * live_mask[:, None, None])
        .reshape(1, tokens, local_heads * P_SIZE)
        .astype(jnp.bfloat16)
    )
    return (gated, end_state[None, None])


def solution(mesh):
    return jax.shard_map(
        on_device,
        mesh=mesh,
        in_specs=(
            P("req", "ctx", "head"),
            P("req", "ctx", None),
            P("req", "ctx", "head"),
            P("req", "head", "ctx"),
            P("head"),
            P("head"),
            P("head"),
            P(None, "head"),
            P(),
            P(("ctx", "req"), "head", None, None),
            P(("ctx", "req"), None, "head"),
            P("req", None, None),
            P(None, "head"),
            P(),
        ),
        out_specs=(P("req", "ctx", "head"), P("req", "ctx", "head", None, None)),
        check_vma=False,
    )
```
